32 devices in a mesh: sub: 2 (over x), section: 4 (over y, core), iface: 4 (over z).
Axes of the slice: x: 2, y: 2, z: 4, core: 2. Of those that a mesh axis runs over, the one named last changes fastest.
Arguments:
- previous: float32 [4, 512, 128], P('section', ('sub', 'iface')), may hold values from -6 to 6
- right_side: float32 [4, 512, 128], P('section', ('sub', 'iface')), may hold values from -96 to 96
- precond: bfloat16 [4, 8, 64, 64], P('section', ('sub', 'iface')), may hold values from -1 to 1
- couple: bfloat16 [4, 8, 64, 64], P('section', ('sub', 'iface')), may hold values from -1.5 to 1.5
- block_ids: int32 [4, 8, 8], P('section', ('sub', 'iface')), may hold values from 0 to 7, as said below
- iface_matrix: bfloat16 [4, 8, 512, 512], P('section', ('sub', 'iface')), may hold values from -1 to 2.5
- interior_coupling: bfloat16 [4, 8, 2560, 512], P('section', ('sub', 'iface')), may hold values from -0.08300781 to 0.08300781
- inv_interior: bfloat16 [4, 8, 2560, 2560], P('section', ('sub', 'iface')), may hold values from -1 to 2
Outputs:
- temperatures: float32 [4, 512, 128], P('section', ('sub', 'iface'))
The draws below stay inside these ranges and needn't reach their ends.
Inputs may be any that keep to these rules, and one draw needn't show every extreme that they name: `block_ids`: each subdomain lists 8 different blocks, and each block of a section is listed by exactly 8 subdomains.
All inputs are finite; a program needn't handle non-finite values.
Results may differ from the reference program's by a relative error of at most 0.0018.
Values may be sent and summed in bfloat16 or wider, within the bound.
No kernel may reach another device: no remote copies, remote signals or barrier semaphores. Data moves between devices by JAX's collectives and lax.ppermute only.
A program may use at most 128 MiB of HBM per device.

```python
import math
import jax
import jax.numpy as jnp
from jax import lax

IB = 64
K = 8
NI = 2560
LOAD = 128
SWEEPS = 4
SECTIONS = 4
NSUBS = 8
NB = 8
KB = 512
NODES = 512


def draw_block_ids(key, part):

    def one_section(index):
        section_key = jax.random.fold_in(jax.random.fold_in(key, 6151), index)
        order_key, offset_key = jax.random.split(section_key)
        starts = jax.random.permutation(order_key, NB).astype(jnp.int32)
        offsets = jax.random.permutation(offset_key, NB).astype(jnp.int32)[:K]
        return (starts[:, None] + offsets[None, :]) % NB
    return lax.map(one_section, jnp.arange(SECTIONS)).astype(jnp.int32)


def draw_iface_matrix(key, part):

    def one_block(index):
        sub_key = jax.random.fold_in(key, index)
        diag_key, off_key = jax.random.split(sub_key)
        diag_vals = jax.random.uniform(diag_key, (KB, 1), jnp.float32, 1.0, 2.0)
        off_vals = jnp.clip(jax.random.normal(off_key, (KB, KB), jnp.float32), -6.0, 6.0) * (0.4 / math.sqrt(KB))
        return jnp.eye(KB, dtype=jnp.float32) * diag_vals + off_vals
    blocks = lax.map(one_block, jnp.arange(SECTIONS * NSUBS))
    return blocks.reshape(SECTIONS, NSUBS, KB, KB).astype(jnp.bfloat16)


def draw_inv_interior(key, part):

    def one_block(index):
        sub_key = jax.random.fold_in(key, index + 7919)
        diag_key, off_key = jax.random.split(sub_key)
        diag_vals = jax.random.uniform(diag_key, (NI, 1), jnp.float32, 0.6, 1.4)
        off_vals = jnp.clip(jax.random.normal(off_key, (NI, NI), jnp.float32), -6.0, 6.0) * (0.3 / math.sqrt(NI))
        return jnp.eye(NI, dtype=jnp.float32) * diag_vals + off_vals
    blocks = lax.map(one_block, jnp.arange(SECTIONS * NSUBS))
    return blocks.reshape(SECTIONS, NSUBS, NI, NI).astype(jnp.bfloat16)


def draw_precond(key, part):
    diag_key, off_key = jax.random.split(jax.random.fold_in(key, 104729))
    diag_vals = jax.random.uniform(diag_key, (SECTIONS, NB, IB, 1), jnp.float32, 0.8, 1.2)
    off_vals = jnp.clip(jax.random.normal(off_key, (SECTIONS, NB, IB, IB), jnp.float32), -6.0, 6.0) * (0.2 / math.sqrt(IB))
    scaled = (jnp.eye(IB, dtype=jnp.float32) * diag_vals + off_vals) * (1.0 / (3.0 * K))
    return scaled.astype(jnp.bfloat16)


def level_of(key, dims, cuts, low, largest):
    loudness, own = 1.0, jax.random.fold_in(key, 6)
    for position, blocks in cuts:
        draws = jnp.exp(jax.random.uniform(jax.random.fold_in(own, position), (blocks,), jnp.float32, low / len(cuts), largest / len(cuts)))
        loudness = loudness * jnp.repeat(draws, dims[position] // blocks).reshape([-1 if axis == position else 1 for axis in range(len(dims))])
    return loudness


def centred(rng, extent, deviation, most, cuts=(), held_as=jnp.bfloat16):
    level = level_of(rng, extent, cuts, -0.22, 0.18) if cuts else 1.0
    values = jax.random.normal(rng, extent, jnp.float32) * deviation * level
    return jnp.minimum(jnp.maximum(values, -most), most).astype(held_as)


def setup_inputs(seed: int = 0) -> dict:
    seeds = jax.random.split(jax.random.key(seed), 9)
    previous = centred(seeds[0], (SECTIONS, NODES, LOAD), 1.0, 6.0, ((0, 4), (1, 8)), jnp.float32)
    right_side = centred(seeds[1], (SECTIONS, NODES, LOAD), (2 * K), 96.0, ((0, 4), (1, 8)), jnp.float32)
    precond = draw_precond(jax.random.fold_in(seeds[8], 71), 0)
    couple = centred(seeds[3], (SECTIONS, NB, IB, IB), (0.25 * K / IB ** 0.5), 1.5, ((0, 4), (1, 8)))
    block_ids = draw_block_ids(jax.random.fold_in(seeds[8], 71), 0)
    iface_matrix = draw_iface_matrix(jax.random.fold_in(seeds[8], 71), 0)
    interior_coupling = centred(seeds[6], (SECTIONS, NSUBS, NI, KB), (0.7 / NI ** 0.5), 0.08300781, ((0, 4), (1, 8)))
    inv_interior = draw_inv_interior(jax.random.fold_in(seeds[8], 71), 0)
    return dict(previous=previous, right_side=right_side, precond=precond, couple=couple, block_ids=block_ids, iface_matrix=iface_matrix, interior_coupling=interior_coupling, inv_interior=inv_interior)


def subdomain_term(item_tuple):
    sub_rows, boundary, coupled, inverse = item_tuple
    interior_in = jnp.dot(coupled, sub_rows, preferred_element_type=jnp.float32).astype(jnp.bfloat16)
    interior_out = jnp.dot(inverse, interior_in, preferred_element_type=jnp.float32).astype(jnp.bfloat16)
    pulled_back = lax.dot_general(coupled, interior_out, (((0,), (0,)), ((), ())), preferred_element_type=jnp.float32)
    return jnp.dot(boundary, sub_rows, preferred_element_type=jnp.float32) - pulled_back


def pick_rows(section_vals, section_ids):
    return jnp.take(section_vals, section_ids.reshape(-1), axis=0)


def add_rows(section_terms, section_ids):
    return jnp.zeros((NB, IB, LOAD), jnp.float32).at[section_ids.reshape(-1)].add(section_terms)


def reference(previous, right_side, precond, couple, block_ids, iface_matrix, interior_coupling, inv_interior):
    highest = lax.Precision.HIGHEST
    temps_now = previous.reshape(SECTIONS, NB, IB, LOAD)
    rhs_all = right_side.reshape(SECTIONS, NB, IB, LOAD)
    precond_f = precond.astype(jnp.float32)
    couple_f = couple.astype(jnp.float32)
    bound_all = iface_matrix.reshape(SECTIONS * NSUBS, K * IB, K * IB)
    coupled_all = interior_coupling.reshape(SECTIONS * NSUBS, NI, K * IB)
    inverse_all = inv_interior.reshape(SECTIONS * NSUBS, NI, NI)
    for sweep_index in range(SWEEPS):
        rounded = temps_now.astype(jnp.bfloat16)
        sub_rows = jax.vmap(pick_rows)(rounded, block_ids).reshape(SECTIONS * NSUBS, K * IB, LOAD)
        sub_terms = lax.map(subdomain_term, (sub_rows, bound_all, coupled_all, inverse_all))
        sub_terms = sub_terms.reshape(SECTIONS, NSUBS * K, IB, LOAD)
        assembled = jax.vmap(add_rows)(sub_terms, block_ids)
        upper_terms = jnp.einsum("sbij,sbil->sbjl", couple_f, temps_now, precision=highest)
        fresh = []
        for section_pos in range(SECTIONS):
            residual_now = rhs_all[section_pos] - assembled[section_pos]
            if section_pos > 0:
                residual_now = residual_now - jnp.einsum("bij,bjl->bil", couple_f[section_pos], fresh[section_pos - 1], precision=highest)
            if section_pos + 1 < SECTIONS:
                residual_now = residual_now - upper_terms[section_pos + 1]
            fresh.append(temps_now[section_pos] + jnp.einsum("bij,bjl->bil", precond_f[section_pos], residual_now, precision=highest))
        temps_now = jnp.stack(fresh)
    return temps_now.reshape(SECTIONS, NB * IB, LOAD)
```

```python
import jax
import jax.numpy as jnp
from jax import lax
from jax.sharding import PartitionSpec as P

SWEEPS = 4
OWNERS = ("sub", "iface")


def split_bf16(value):
    high = value.astype(jnp.bfloat16)
    low = (value - high.astype(jnp.float32)).astype(jnp.bfloat16)
    return high, low


def gather_along(block, axis):
    count = lax.axis_size(axis)
    copies = jnp.broadcast_to(block[None], (count,) + block.shape)
    return lax.all_to_all(copies, axis, 0, 0, tiled=True)


def schur_rows(block_list, boundary, coupled, inverse, owners):
    picks = block_list.shape[0]
    block_nodes = boundary.shape[0] // picks
    solved = jnp.dot(inverse, coupled, preferred_element_type=jnp.float32)
    solved_hi, solved_lo = split_bf16(solved)
    contract = (((0,), (0,)), ((), ()))
    pulled = lax.dot_general(coupled, solved_hi, contract, preferred_element_type=jnp.float32)
    pulled = pulled + lax.dot_general(coupled, solved_lo, contract, preferred_element_type=jnp.float32)
    schur = boundary.astype(jnp.float32) - pulled
    listed = block_list[None, :] == jnp.arange(owners, dtype=jnp.int32)[:, None]
    slot = jnp.where(jnp.any(listed, axis=1), jnp.argmax(listed, axis=1), picks)
    padded = jnp.pad(
        schur.reshape(picks, block_nodes, picks, block_nodes), ((0, 1), (0, 0), (0, 1), (0, 0))
    )
    spread = jnp.take(jnp.take(padded, slot, axis=0), slot, axis=2)
    spread = spread.reshape(owners, block_nodes, owners * block_nodes)
    received = lax.all_to_all(spread, OWNERS, 0, 0, tiled=True)
    return jnp.sum(received, axis=0)


def chain_weights(precond_f, couple_f):
    highest = lax.Precision.HIGHEST
    sections, block_nodes = precond_f.shape[0], precond_f.shape[1]
    step = jnp.einsum("gij,gjk->gik", precond_f, couple_f, precision=highest)
    eye = jnp.eye(block_nodes, dtype=jnp.float32)
    zero = jnp.zeros_like(eye)
    rows = []
    for h in range(sections):
        if h == 0:
            row = [eye] + [zero] * (sections - 1)
        else:
            row = [-jnp.dot(step[h], rows[h - 1][k], precision=highest) for k in range(h)]
            row = row + [eye] + [zero] * (sections - 1 - h)
        rows.append(row)
    return jnp.stack([jnp.stack(row) for row in rows])


def body(
    previous, right_side, precond, couple, block_ids, iface_matrix, interior_coupling, inv_interior
):
    highest = lax.Precision.HIGHEST
    section_pos = lax.axis_index("section")
    sections = lax.axis_size("section")
    owners = lax.axis_size(OWNERS)
    block_nodes = previous.shape[1]
    load_count = previous.shape[2]
    nodes = owners * block_nodes

    tables = jnp.concatenate(
        [previous[0], precond[0, 0].astype(jnp.float32), couple[0, 0].astype(jnp.float32)],
        axis=1,
    )
    tables = gather_along(tables, "section")
    start_all = tables[:, :, :load_count]
    precond_all = tables[:, :, load_count : load_count + block_nodes]
    couple_all = tables[:, :, load_count + block_nodes :]
    weights = chain_weights(precond_all, couple_all)
    above_pos = jnp.minimum(section_pos + 1, sections - 1)
    has_above = section_pos + 1 < sections
    weights_mine = weights[section_pos]
    weights_above = weights[above_pos]
    precond_mine = precond[0, 0].astype(jnp.float32)
    couple_above = couple_all[above_pos]

    rows = schur_rows(
        block_ids[0, 0], iface_matrix[0, 0], interior_coupling[0, 0], inv_interior[0, 0], owners
    )
    rows_hi, rows_lo = split_bf16(rows)

    temps_mine = previous[0]
    temps_above = start_all[above_pos]
    rhs = right_side[0]
    for sweep_index in range(SWEEPS):
        rounded = gather_along(temps_mine.astype(jnp.bfloat16), OWNERS).reshape(nodes, load_count)
        assembled = jnp.dot(rows_hi, rounded, preferred_element_type=jnp.float32) + jnp.dot(
            rows_lo, rounded, preferred_element_type=jnp.float32
        )
        from_above = jnp.einsum("ij,il->jl", couple_above, temps_above, precision=highest)
        from_above = jnp.where(has_above, from_above, 0.0)
        residual = rhs - assembled - from_above
        update = temps_mine + jnp.dot(precond_mine, residual, precision=highest)
        updates = gather_along(update, "section")
        temps_mine = jnp.einsum("kij,kjl->il", weights_mine, updates, precision=highest)
        temps_above = jnp.einsum("kij,kjl->il", weights_above, updates, precision=highest)
    return temps_mine[None]


def solution(mesh):
    in_specs = (
        P("section", OWNERS, None),
        P("section", OWNERS, None),
        P("section", OWNERS, None, None),
        P("section", OWNERS, None, None),
        P("section", OWNERS, None),
        P("section", OWNERS, None, None),
        P("section", OWNERS, None, None),
        P("section", OWNERS, None, None),
    )
    out_specs = P("section", OWNERS, None)
    return jax.shard_map(body, mesh=mesh, in_specs=in_specs, out_specs=out_specs, check_vma=False)
```

```python
import jax
import jax.numpy as jnp
from jax import lax
from jax.sharding import PartitionSpec as P

SWEEPS = 4
OWNERS = ("sub", "iface")


def split_bf16(value):
    high = lax.reduce_precision(value, exponent_bits=8, mantissa_bits=7)
    return high.astype(jnp.bfloat16), (value - high).astype(jnp.bfloat16)


def gather_along(block, axis):
    count = lax.axis_size(axis)
    copies = jnp.broadcast_to(block[None], (count,) + block.shape)
    return lax.all_to_all(copies, axis, 0, 0, tiled=True)


def schur_rows(block_list, boundary, coupled, inverse, owners):
    picks = block_list.shape[0]
    block_nodes = boundary.shape[0] // picks
    solved = jnp.dot(inverse, coupled, preferred_element_type=jnp.float32)
    solved_hi, solved_lo = split_bf16(solved)
    contract = (((0,), (0,)), ((), ()))
    pulled = lax.dot_general(coupled, solved_hi, contract, preferred_element_type=jnp.float32)
    pulled = pulled + lax.dot_general(coupled, solved_lo, contract, preferred_element_type=jnp.float32)
    schur = boundary.astype(jnp.float32) - pulled
    node = jnp.arange(owners * block_nodes, dtype=jnp.int32)
    sub = jnp.arange(picks * block_nodes, dtype=jnp.int32)
    target = jnp.repeat(block_list, block_nodes) * block_nodes + sub % block_nodes
    place = (target[:, None] == node[None, :]).astype(jnp.bfloat16)
    schur_hi, schur_lo = split_bf16(schur)
    contract_rows = (((0,), (0,)), ((), ()))
    spread = jnp.zeros((owners * block_nodes, owners * block_nodes), jnp.float32)
    for part in (schur_hi, schur_lo):
        moved = lax.dot_general(place, part, contract_rows, preferred_element_type=jnp.float32)
        spread = spread + jnp.dot(
            moved.astype(jnp.bfloat16), place, preferred_element_type=jnp.float32
        )
    spread = spread.reshape(owners, block_nodes, owners * block_nodes)
    received = lax.all_to_all(spread, OWNERS, 0, 0, tiled=True)
    return jnp.sum(received, axis=0)


def chain_weights(precond_f, couple_f):
    highest = lax.Precision.HIGHEST
    sections, block_nodes = precond_f.shape[0], precond_f.shape[1]
    step = jnp.einsum("gij,gjk->gik", precond_f, couple_f, precision=highest)
    eye = jnp.eye(block_nodes, dtype=jnp.float32)
    zero = jnp.zeros_like(eye)
    rows = []
    for h in range(sections):
        if h == 0:
            row = [eye] + [zero] * (sections - 1)
        else:
            row = [-jnp.dot(step[h], rows[h - 1][k], precision=highest) for k in range(h)]
            row = row + [eye] + [zero] * (sections - 1 - h)
        rows.append(row)
    return jnp.stack([jnp.stack(row) for row in rows])


def body(
    previous, right_side, precond, couple, block_ids, iface_matrix, interior_coupling, inv_interior
):
    highest = lax.Precision.HIGHEST
    section_pos = lax.axis_index("section")
    sections = lax.axis_size("section")
    owners = lax.axis_size(OWNERS)
    block_nodes = previous.shape[1]
    load_count = previous.shape[2]
    nodes = owners * block_nodes

    tables = jnp.concatenate(
        [previous[0], precond[0, 0].astype(jnp.float32), couple[0, 0].astype(jnp.float32)],
        axis=1,
    )
    tables = gather_along(tables, "section")
    start_all = tables[:, :, :load_count]
    precond_all = tables[:, :, load_count : load_count + block_nodes]
    couple_all = tables[:, :, load_count + block_nodes :]
    weights = chain_weights(precond_all, couple_all)
    above_pos = jnp.minimum(section_pos + 1, sections - 1)
    has_above = section_pos + 1 < sections
    weights_mine = weights[section_pos]
    weights_above = weights[above_pos]
    precond_mine = precond[0, 0].astype(jnp.float32)
    couple_above = couple_all[above_pos]

    rows = schur_rows(
        block_ids[0, 0], iface_matrix[0, 0], interior_coupling[0, 0], inv_interior[0, 0], owners
    )
    rows_hi, rows_lo = split_bf16(rows)

    temps_mine = previous[0]
    temps_above = start_all[above_pos]
    rhs = right_side[0]
    for sweep_index in range(SWEEPS):
        rounded = gather_along(temps_mine.astype(jnp.bfloat16), OWNERS).reshape(nodes, load_count)
        assembled = jnp.dot(rows_hi, rounded, preferred_element_type=jnp.float32) + jnp.dot(
            rows_lo, rounded, preferred_element_type=jnp.float32
        )
        from_above = jnp.einsum("ij,il->jl", couple_above, temps_above, precision=highest)
        from_above = jnp.where(has_above, from_above, 0.0)
        residual = rhs - assembled - from_above
        update = temps_mine + jnp.dot(precond_mine, residual, precision=highest)
        updates = gather_along(update, "section")
        temps_mine = jnp.einsum("kij,kjl->il", weights_mine, updates, precision=highest)
        temps_above = jnp.einsum("kij,kjl->il", weights_above, updates, precision=highest)
    return temps_mine[None]


def solution(mesh):
    in_specs = (
        P("section", OWNERS, None),
        P("section", OWNERS, None),
        P("section", OWNERS, None, None),
        P("section", OWNERS, None, None),
        P("section", OWNERS, None),
        P("section", OWNERS, None, None),
        P("section", OWNERS, None, None),
        P("section", OWNERS, None, None),
    )
    out_specs = P("section", OWNERS, None)
    return jax.shard_map(body, mesh=mesh, in_specs=in_specs, out_specs=out_specs, check_vma=False)
```

```python
import jax
import jax.numpy as jnp
from jax import lax
from jax.sharding import PartitionSpec as P

SWEEPS = 4
OWNERS = ("sub", "iface")


def split_bf16(value):
    high = lax.reduce_precision(value, exponent_bits=8, mantissa_bits=7)
    return high.astype(jnp.bfloat16), (value - high).astype(jnp.bfloat16)


def gather_along(block, axis):
    count = lax.axis_size(axis)
    copies = jnp.broadcast_to(block[None], (count,) + block.shape)
    return lax.all_to_all(copies, axis, 0, 0, tiled=True)


def schur_rows(block_list, boundary, coupled, inverse, owners):
    picks = block_list.shape[0]
    block_nodes = boundary.shape[0] // picks
    solved = jnp.dot(inverse, coupled, preferred_element_type=jnp.float32)
    solved_hi, solved_lo = split_bf16(solved)
    contract = (((0,), (0,)), ((), ()))
    pulled = lax.dot_general(coupled, solved_hi, contract, preferred_element_type=jnp.float32)
    pulled = pulled + lax.dot_general(coupled, solved_lo, contract, preferred_element_type=jnp.float32)
    schur = boundary.astype(jnp.float32) - pulled
    node = jnp.arange(owners * block_nodes, dtype=jnp.int32)
    sub = jnp.arange(picks * block_nodes, dtype=jnp.int32)
    target = jnp.repeat(block_list, block_nodes) * block_nodes + sub % block_nodes
    place = (target[:, None] == node[None, :]).astype(jnp.bfloat16)
    schur_hi, schur_lo = split_bf16(schur)
    contract_rows = (((0,), (0,)), ((), ()))
    spread = jnp.zeros((owners * block_nodes, owners * block_nodes), jnp.float32)
    for part in (schur_hi, schur_lo):
        moved = lax.dot_general(place, part, contract_rows, preferred_element_type=jnp.float32)
        spread = spread + jnp.dot(
            moved.astype(jnp.bfloat16), place, preferred_element_type=jnp.float32
        )
    return spread.reshape(owners, block_nodes, owners * block_nodes)


def chain_weights(precond_f, couple_f):
    highest = lax.Precision.HIGHEST
    sections, block_nodes = precond_f.shape[0], precond_f.shape[1]
    step = jnp.einsum("gij,gjk->gik", precond_f, couple_f, precision=highest)
    eye = jnp.eye(block_nodes, dtype=jnp.float32)
    zero = jnp.zeros_like(eye)
    rows = []
    for h in range(sections):
        if h == 0:
            row = [eye] + [zero] * (sections - 1)
        else:
            row = [-jnp.dot(step[h], rows[h - 1][k], precision=highest) for k in range(h)]
            row = row + [eye] + [zero] * (sections - 1 - h)
        rows.append(row)
    return jnp.stack([jnp.stack(row) for row in rows])


def body(
    previous, right_side, precond, couple, block_ids, iface_matrix, interior_coupling, inv_interior
):
    high = lax.Precision.HIGH
    section_pos = lax.axis_index("section")
    sections = lax.axis_size("section")
    owners = lax.axis_size(OWNERS)
    block_nodes = previous.shape[1]
    load_count = previous.shape[2]
    nodes = owners * block_nodes

    tables = jnp.concatenate(
        [previous[0], precond[0, 0].astype(jnp.float32), couple[0, 0].astype(jnp.float32)],
        axis=1,
    )
    tables = gather_along(tables, "section")
    start_all = tables[:, :, :load_count]
    precond_all = tables[:, :, load_count : load_count + block_nodes]
    couple_all = tables[:, :, load_count + block_nodes :]
    weights = chain_weights(precond_all, couple_all)
    above_pos = jnp.minimum(section_pos + 1, sections - 1)
    has_above = section_pos + 1 < sections
    weights_mine = weights[section_pos]
    weights_above = weights[above_pos]
    precond_mine = precond[0, 0].astype(jnp.float32)
    couple_above = couple_all[above_pos]

    first_rounded = gather_along(previous[0].astype(jnp.bfloat16), OWNERS)
    spread = schur_rows(
        block_ids[0, 0], iface_matrix[0, 0], interior_coupling[0, 0], inv_interior[0, 0], owners
    )
    first_rounded, tables, spread = lax.optimization_barrier((first_rounded, tables, spread))
    rows = jnp.sum(lax.all_to_all(spread, OWNERS, 0, 0, tiled=True), axis=0)
    rows_hi, rows_lo = split_bf16(rows)

    temps_mine = previous[0]
    temps_above = start_all[above_pos]
    rhs = right_side[0]
    for sweep_index in range(SWEEPS):
        if sweep_index == 0:
            rounded = first_rounded
        else:
            rounded = gather_along(temps_mine.astype(jnp.bfloat16), OWNERS)
        rounded = rounded.reshape(nodes, load_count)
        assembled = jnp.dot(rows_hi, rounded, preferred_element_type=jnp.float32) + jnp.dot(
            rows_lo, rounded, preferred_element_type=jnp.float32
        )
        from_above = jnp.einsum("ij,il->jl", couple_above, temps_above, precision=high)
        from_above = jnp.where(has_above, from_above, 0.0)
        residual = rhs - assembled - from_above
        update = temps_mine + jnp.dot(precond_mine, residual, precision=high)
        updates = gather_along(update, "section")
        temps_mine = jnp.einsum("kij,kjl->il", weights_mine, updates, precision=high)
        temps_above = jnp.einsum("kij,kjl->il", weights_above, updates, precision=high)
    return temps_mine[None]


def solution(mesh):
    in_specs = (
        P("section", OWNERS, None),
        P("section", OWNERS, None),
        P("section", OWNERS, None, None),
        P("section", OWNERS, None, None),
        P("section", OWNERS, None),
        P("section", OWNERS, None, None),
        P("section", OWNERS, None, None),
        P("section", OWNERS, None, None),
    )
    out_specs = P("section", OWNERS, None)
    return jax.shard_map(body, mesh=mesh, in_specs=in_specs, out_specs=out_specs, check_vma=False)
```

```python
import jax
import jax.numpy as jnp
from jax import lax
from jax.sharding import PartitionSpec as P

SWEEPS = 4
OWNERS = ("sub", "iface")


def split_bf16(value):
    high = lax.reduce_precision(value, exponent_bits=8, mantissa_bits=7)
    return high.astype(jnp.bfloat16), (value - high).astype(jnp.bfloat16)


def gather_along(block, axis):
    count = lax.axis_size(axis)
    copies = jnp.broadcast_to(block[None], (count,) + block.shape)
    return lax.all_to_all(copies, axis, 0, 0, tiled=True)


def schur_rows(block_list, boundary, coupled, inverse, owners):
    picks = block_list.shape[0]
    block_nodes = boundary.shape[0] // picks
    nodes = owners * block_nodes
    contract = (((0,), (0,)), ((), ()))
    node = jnp.arange(nodes, dtype=jnp.int32)
    slot_node = jnp.arange(picks * block_nodes, dtype=jnp.int32)
    target = jnp.repeat(block_list, block_nodes) * block_nodes + slot_node % block_nodes
    place = (target[:, None] == node[None, :]).astype(jnp.bfloat16)

    def moved(matrix):
        rows = lax.dot_general(place, matrix, contract, preferred_element_type=jnp.float32)
        return jnp.dot(rows.astype(jnp.bfloat16), place, preferred_element_type=jnp.float32)

    if picks == owners:
        coupled = jnp.dot(coupled, place, preferred_element_type=jnp.float32).astype(jnp.bfloat16)
        boundary = moved(boundary)
    solved = jnp.dot(inverse, coupled, preferred_element_type=jnp.float32)
    solved_hi, solved_lo = split_bf16(solved)
    pulled = lax.dot_general(coupled, solved_hi, contract, preferred_element_type=jnp.float32)
    pulled = pulled + lax.dot_general(coupled, solved_lo, contract, preferred_element_type=jnp.float32)
    schur = boundary.astype(jnp.float32) - pulled
    if picks != owners:
        schur_hi, schur_lo = split_bf16(schur)
        schur = moved(schur_hi) + moved(schur_lo)
    return schur.reshape(owners, block_nodes, nodes)


def chain_weights(precond_f, couple_f):
    highest = lax.Precision.HIGHEST
    sections, block_nodes = precond_f.shape[0], precond_f.shape[1]
    step = jnp.einsum("gij,gjk->gik", precond_f, couple_f, precision=highest)
    eye = jnp.eye(block_nodes, dtype=jnp.float32)
    zero = jnp.zeros_like(eye)
    rows = []
    for h in range(sections):
        if h == 0:
            row = [eye] + [zero] * (sections - 1)
        else:
            row = [-jnp.dot(step[h], rows[h - 1][k], precision=highest) for k in range(h)]
            row = row + [eye] + [zero] * (sections - 1 - h)
        rows.append(row)
    return jnp.stack([jnp.stack(row) for row in rows])


def body(
    previous, right_side, precond, couple, block_ids, iface_matrix, interior_coupling, inv_interior
):
    high = lax.Precision.HIGH
    section_pos = lax.axis_index("section")
    sections = lax.axis_size("section")
    owners = lax.axis_size(OWNERS)
    block_nodes = previous.shape[1]
    load_count = previous.shape[2]
    nodes = owners * block_nodes

    tables = jnp.concatenate(
        [previous[0], precond[0, 0].astype(jnp.float32), couple[0, 0].astype(jnp.float32)],
        axis=1,
    )
    tables = gather_along(tables, "section")
    start_all = tables[:, :, :load_count]
    precond_all = tables[:, :, load_count : load_count + block_nodes]
    couple_all = tables[:, :, load_count + block_nodes :]
    weights = chain_weights(precond_all, couple_all)
    above_pos = jnp.minimum(section_pos + 1, sections - 1)
    has_above = section_pos + 1 < sections
    weights_mine = weights[section_pos]
    weights_above = weights[above_pos]
    precond_mine = precond[0, 0].astype(jnp.float32)
    couple_above = couple_all[above_pos]

    first_rounded = gather_along(previous[0].astype(jnp.bfloat16), OWNERS)
    spread = schur_rows(
        block_ids[0, 0], iface_matrix[0, 0], interior_coupling[0, 0], inv_interior[0, 0], owners
    )
    first_rounded, tables, spread = lax.optimization_barrier((first_rounded, tables, spread))
    rows = jnp.sum(lax.all_to_all(spread, OWNERS, 0, 0, tiled=True), axis=0)
    rows_hi, rows_lo = split_bf16(jnp.dot(precond_mine, rows, precision=lax.Precision.HIGHEST))

    temps_mine = previous[0]
    temps_above = start_all[above_pos]
    rhs = right_side[0]
    for sweep_index in range(SWEEPS):
        if sweep_index == 0:
            rounded = first_rounded
        else:
            rounded = gather_along(temps_mine.astype(jnp.bfloat16), OWNERS)
        rounded = rounded.reshape(nodes, load_count)
        from_above = jnp.einsum("ij,il->jl", couple_above, temps_above, precision=high)
        from_above = jnp.where(has_above, from_above, 0.0)
        known = temps_mine + jnp.dot(precond_mine, rhs - from_above, precision=high)
        update = known - (
            jnp.dot(rows_hi, rounded, preferred_element_type=jnp.float32)
            + jnp.dot(rows_lo, rounded, preferred_element_type=jnp.float32)
        )
        updates = gather_along(update, "section")
        temps_mine = jnp.einsum("kij,kjl->il", weights_mine, updates, precision=high)
        temps_above = jnp.einsum("kij,kjl->il", weights_above, updates, precision=high)
    return temps_mine[None]


def solution(mesh):
    in_specs = (
        P("section", OWNERS, None),
        P("section", OWNERS, None),
        P("section", OWNERS, None, None),
        P("section", OWNERS, None, None),
        P("section", OWNERS, None),
        P("section", OWNERS, None, None),
        P("section", OWNERS, None, None),
        P("section", OWNERS, None, None),
    )
    out_specs = P("section", OWNERS, None)
    return jax.shard_map(body, mesh=mesh, in_specs=in_specs, out_specs=out_specs, check_vma=False)
```

```python
import jax
import jax.numpy as jnp
from jax import lax
from jax.sharding import PartitionSpec as P

SWEEPS = 4
OWNERS = ("sub", "iface")


def split_bf16(value):
    high = lax.reduce_precision(value, exponent_bits=8, mantissa_bits=7)
    return high.astype(jnp.bfloat16), (value - high).astype(jnp.bfloat16)


def gather_along(block, axis):
    count = lax.axis_size(axis)
    copies = jnp.broadcast_to(block[None], (count,) + block.shape)
    return lax.all_to_all(copies, axis, 0, 0, tiled=True)


def schur_rows(block_list, boundary, coupled, inverse, owners):
    picks = block_list.shape[0]
    block_nodes = boundary.shape[0] // picks
    nodes = owners * block_nodes
    contract = (((0,), (0,)), ((), ()))
    node = jnp.arange(nodes, dtype=jnp.int32)
    slot_node = jnp.arange(picks * block_nodes, dtype=jnp.int32)
    target = jnp.repeat(block_list, block_nodes) * block_nodes + slot_node % block_nodes
    place = (target[:, None] == node[None, :]).astype(jnp.bfloat16)

    def moved(matrix):
        rows = lax.dot_general(place, matrix, contract, preferred_element_type=jnp.float32)
        return jnp.dot(rows.astype(jnp.bfloat16), place, preferred_element_type=jnp.float32)

    if picks == owners:
        coupled = jnp.dot(coupled, place, preferred_element_type=jnp.float32).astype(jnp.bfloat16)
        boundary = moved(boundary)
    solved = jnp.dot(inverse, coupled, preferred_element_type=jnp.float32)
    solved_hi, solved_lo = split_bf16(solved)
    pulled = lax.dot_general(coupled, solved_hi, contract, preferred_element_type=jnp.float32)
    pulled = pulled + lax.dot_general(coupled, solved_lo, contract, preferred_element_type=jnp.float32)
    schur = boundary.astype(jnp.float32) - pulled
    if picks != owners:
        schur_hi, schur_lo = split_bf16(schur)
        schur = moved(schur_hi) + moved(schur_lo)
    return schur.reshape(owners, block_nodes, nodes)


def chain_weights(precond_f, couple_f):
    highest = lax.Precision.HIGHEST
    sections, block_nodes = precond_f.shape[0], precond_f.shape[1]
    step = jnp.einsum("gij,gjk->gik", precond_f, couple_f, precision=highest)
    eye = jnp.eye(block_nodes, dtype=jnp.float32)
    zero = jnp.zeros_like(eye)
    rows = []
    for h in range(sections):
        if h == 0:
            row = [eye] + [zero] * (sections - 1)
        else:
            row = [-jnp.dot(step[h], rows[h - 1][k], precision=highest) for k in range(h)]
            row = row + [eye] + [zero] * (sections - 1 - h)
        rows.append(row)
    return jnp.stack([jnp.stack(row) for row in rows])


def body(
    previous, right_side, precond, couple, block_ids, iface_matrix, interior_coupling, inv_interior
):
    high = lax.Precision.HIGH
    section_pos = lax.axis_index("section")
    sections = lax.axis_size("section")
    owners = lax.axis_size(OWNERS)
    block_nodes = previous.shape[1]
    load_count = previous.shape[2]
    nodes = owners * block_nodes

    tables = jnp.concatenate(
        [previous[0], precond[0, 0].astype(jnp.float32), couple[0, 0].astype(jnp.float32)],
        axis=1,
    )
    first_rounded = gather_along(previous[0].astype(jnp.bfloat16), OWNERS)
    first_rounded, tables = lax.optimization_barrier((first_rounded, tables))
    tables = gather_along(tables, "section")
    start_all = tables[:, :, :load_count]
    precond_all = tables[:, :, load_count : load_count + block_nodes]
    couple_all = tables[:, :, load_count + block_nodes :]
    weights = chain_weights(precond_all, couple_all)
    above_pos = jnp.minimum(section_pos + 1, sections - 1)
    has_above = section_pos + 1 < sections
    weights_mine = weights[section_pos]
    weights_above = weights[above_pos]
    precond_mine = precond[0, 0].astype(jnp.float32)
    couple_above = couple_all[above_pos]

    spread = schur_rows(
        block_ids[0, 0], iface_matrix[0, 0], interior_coupling[0, 0], inv_interior[0, 0], owners
    )
    tables, spread = lax.optimization_barrier((tables, spread))
    rows = jnp.sum(lax.all_to_all(spread, OWNERS, 0, 0, tiled=True), axis=0)
    rows_hi, rows_lo = split_bf16(jnp.dot(precond_mine, rows, precision=lax.Precision.HIGHEST))

    temps_mine = previous[0]
    temps_above = start_all[above_pos]
    rhs = right_side[0]
    for sweep_index in range(SWEEPS):
        if sweep_index == 0:
            rounded = first_rounded
        else:
            rounded = gather_along(temps_mine.astype(jnp.bfloat16), OWNERS)
        rounded = rounded.reshape(nodes, load_count)
        from_above = jnp.einsum("ij,il->jl", couple_above, temps_above, precision=high)
        from_above = jnp.where(has_above, from_above, 0.0)
        known = temps_mine + jnp.dot(precond_mine, rhs - from_above, precision=high)
        update = known - (
            jnp.dot(rows_hi, rounded, preferred_element_type=jnp.float32)
            + jnp.dot(rows_lo, rounded, preferred_element_type=jnp.float32)
        )
        updates = gather_along(update, "section")
        temps_mine = jnp.einsum("kij,kjl->il", weights_mine, updates, precision=high)
        temps_above = jnp.einsum("kij,kjl->il", weights_above, updates, precision=high)
    return temps_mine[None]


def solution(mesh):
    in_specs = (
        P("section", OWNERS, None),
        P("section", OWNERS, None),
        P("section", OWNERS, None, None),
        P("section", OWNERS, None, None),
        P("section", OWNERS, None),
        P("section", OWNERS, None, None),
        P("section", OWNERS, None, None),
        P("section", OWNERS, None, None),
    )
    out_specs = P("section", OWNERS, None)
    return jax.shard_map(body, mesh=mesh, in_specs=in_specs, out_specs=out_specs, check_vma=False)
```

```python
import jax
import jax.numpy as jnp
from jax import lax
from jax.sharding import PartitionSpec as P

SWEEPS = 4
OWNERS = ("sub", "iface")


def split_bf16(value):
    high = lax.reduce_precision(value, exponent_bits=8, mantissa_bits=7)
    return high.astype(jnp.bfloat16), (value - high).astype(jnp.bfloat16)


def gather_along(block, axis):
    count = lax.axis_size(axis)
    copies = jnp.broadcast_to(block[None], (count,) + block.shape)
    return lax.all_to_all(copies, axis, 0, 0, tiled=True)


def ring_parts(block, axis):
    count = lax.axis_size(axis)
    parts = [block]
    for distance in range(1, count):
        route = [(i, (i + distance) % count) for i in range(count)]
        parts.append(lax.ppermute(block, axis, route))
    return jnp.stack(parts)


def schur_rows(block_list, boundary, coupled, inverse, owners):
    picks = block_list.shape[0]
    block_nodes = boundary.shape[0] // picks
    nodes = owners * block_nodes
    contract = (((0,), (0,)), ((), ()))
    node = jnp.arange(nodes, dtype=jnp.int32)
    slot_node = jnp.arange(picks * block_nodes, dtype=jnp.int32)
    target = jnp.repeat(block_list, block_nodes) * block_nodes + slot_node % block_nodes
    place = (target[:, None] == node[None, :]).astype(jnp.bfloat16)

    def moved(matrix):
        rows = lax.dot_general(place, matrix, contract, preferred_element_type=jnp.float32)
        return jnp.dot(rows.astype(jnp.bfloat16), place, preferred_element_type=jnp.float32)

    if picks == owners:
        coupled = jnp.dot(coupled, place, preferred_element_type=jnp.float32).astype(jnp.bfloat16)
        boundary = moved(boundary)
    solved = jnp.dot(inverse, coupled, preferred_element_type=jnp.float32)
    solved_hi, solved_lo = split_bf16(solved)
    pulled = lax.dot_general(coupled, solved_hi, contract, preferred_element_type=jnp.float32)
    pulled = pulled + lax.dot_general(coupled, solved_lo, contract, preferred_element_type=jnp.float32)
    schur = boundary.astype(jnp.float32) - pulled
    if picks != owners:
        schur_hi, schur_lo = split_bf16(schur)
        schur = moved(schur_hi) + moved(schur_lo)
    return schur.reshape(owners, block_nodes, nodes)


def chain_weights(precond_f, couple_f):
    highest = lax.Precision.HIGHEST
    sections, block_nodes = precond_f.shape[0], precond_f.shape[1]
    step = jnp.einsum("gij,gjk->gik", precond_f, couple_f, precision=highest)
    eye = jnp.eye(block_nodes, dtype=jnp.float32)
    zero = jnp.zeros_like(eye)
    rows = []
    for h in range(sections):
        if h == 0:
            row = [eye] + [zero] * (sections - 1)
        else:
            row = [-jnp.dot(step[h], rows[h - 1][k], precision=highest) for k in range(h)]
            row = row + [eye] + [zero] * (sections - 1 - h)
        rows.append(row)
    return jnp.stack([jnp.stack(row) for row in rows])


def body(
    previous, right_side, precond, couple, block_ids, iface_matrix, interior_coupling, inv_interior
):
    high = lax.Precision.HIGH
    section_pos = lax.axis_index("section")
    sections = lax.axis_size("section")
    owners = lax.axis_size(OWNERS)
    block_nodes = previous.shape[1]
    load_count = previous.shape[2]
    nodes = owners * block_nodes

    tables = jnp.concatenate(
        [previous[0], precond[0, 0].astype(jnp.float32), couple[0, 0].astype(jnp.float32)],
        axis=1,
    )
    first_rounded = gather_along(previous[0].astype(jnp.bfloat16), OWNERS)
    first_rounded, tables = lax.optimization_barrier((first_rounded, tables))
    tables = gather_along(tables, "section")
    start_all = tables[:, :, :load_count]
    precond_all = tables[:, :, load_count : load_count + block_nodes]
    couple_all = tables[:, :, load_count + block_nodes :]
    weights = chain_weights(precond_all, couple_all)
    above_pos = jnp.minimum(section_pos + 1, sections - 1)
    has_above = section_pos + 1 < sections
    behind = (section_pos - jnp.arange(sections)) % sections
    weights_mine = jnp.take(weights[section_pos], behind, axis=0)
    weights_above = jnp.take(weights[above_pos], behind, axis=0)
    precond_mine = precond[0, 0].astype(jnp.float32)
    couple_above = couple_all[above_pos]

    spread = schur_rows(
        block_ids[0, 0], iface_matrix[0, 0], interior_coupling[0, 0], inv_interior[0, 0], owners
    )
    tables, spread = lax.optimization_barrier((tables, spread))
    rows = jnp.sum(lax.all_to_all(spread, OWNERS, 0, 0, tiled=True), axis=0)
    rows_hi, rows_lo = split_bf16(jnp.dot(precond_mine, rows, precision=lax.Precision.HIGHEST))

    temps_mine = previous[0]
    temps_above = start_all[above_pos]
    rhs = right_side[0]
    for sweep_index in range(SWEEPS):
        if sweep_index == 0:
            rounded = first_rounded
        else:
            rounded = gather_along(temps_mine.astype(jnp.bfloat16), OWNERS)
        rounded = rounded.reshape(nodes, load_count)
        from_above = jnp.einsum("ij,il->jl", couple_above, temps_above, precision=high)
        from_above = jnp.where(has_above, from_above, 0.0)
        known = temps_mine + jnp.dot(precond_mine, rhs - from_above, precision=high)
        update = known - (
            jnp.dot(rows_hi, rounded, preferred_element_type=jnp.float32)
            + jnp.dot(rows_lo, rounded, preferred_element_type=jnp.float32)
        )
        updates = ring_parts(update, "section")
        temps_mine = jnp.einsum("kij,kjl->il", weights_mine, updates, precision=high)
        temps_above = jnp.einsum("kij,kjl->il", weights_above, updates, precision=high)
    return temps_mine[None]


def solution(mesh):
    in_specs = (
        P("section", OWNERS, None),
        P("section", OWNERS, None),
        P("section", OWNERS, None, None),
        P("section", OWNERS, None, None),
        P("section", OWNERS, None),
        P("section", OWNERS, None, None),
        P("section", OWNERS, None, None),
        P("section", OWNERS, None, None),
    )
    out_specs = P("section", OWNERS, None)
    return jax.shard_map(body, mesh=mesh, in_specs=in_specs, out_specs=out_specs, check_vma=False)
```

```python
import jax
import jax.numpy as jnp
from jax import lax
from jax.sharding import PartitionSpec as P

SWEEPS = 4
OWNERS = ("sub", "iface")


def split_bf16(value):
    high = lax.reduce_precision(value, exponent_bits=8, mantissa_bits=7)
    return high.astype(jnp.bfloat16), (value - high).astype(jnp.bfloat16)


def gather_along(block, axis):
    count = lax.axis_size(axis)
    copies = jnp.broadcast_to(block[None], (count,) + block.shape)
    return lax.all_to_all(copies, axis, 0, 0, tiled=True)


def ring_parts(block, axis):
    count = lax.axis_size(axis)
    parts = [block]
    for distance in range(1, count):
        route = [(i, (i + distance) % count) for i in range(count)]
        parts.append(lax.ppermute(block, axis, route))
    return jnp.stack(parts)


def gather_owners(block):
    inner = ring_parts(block, "iface")
    outer = ring_parts(inner, "sub")
    return outer.reshape((-1,) + block.shape)


def ring_owner_order():
    subs, ifaces = lax.axis_size("sub"), lax.axis_size("iface")
    sub_back = (lax.axis_index("sub") - jnp.arange(subs)[:, None]) % subs
    iface_back = (lax.axis_index("iface") - jnp.arange(ifaces)[None, :]) % ifaces
    return (sub_back * ifaces + iface_back).reshape(-1)


def schur_rows(block_list, boundary, coupled, inverse, owners):
    picks = block_list.shape[0]
    block_nodes = boundary.shape[0] // picks
    nodes = owners * block_nodes
    contract = (((0,), (0,)), ((), ()))
    node = jnp.arange(nodes, dtype=jnp.int32)
    slot_node = jnp.arange(picks * block_nodes, dtype=jnp.int32)
    target = jnp.repeat(block_list, block_nodes) * block_nodes + slot_node % block_nodes
    place = (target[:, None] == node[None, :]).astype(jnp.bfloat16)

    def moved(matrix):
        rows = lax.dot_general(place, matrix, contract, preferred_element_type=jnp.float32)
        return jnp.dot(rows.astype(jnp.bfloat16), place, preferred_element_type=jnp.float32)

    if picks == owners:
        coupled = jnp.dot(coupled, place, preferred_element_type=jnp.float32).astype(jnp.bfloat16)
        boundary = moved(boundary)
    solved = jnp.dot(inverse, coupled, preferred_element_type=jnp.float32)
    solved_hi, solved_lo = split_bf16(solved)
    pulled = lax.dot_general(coupled, solved_hi, contract, preferred_element_type=jnp.float32)
    pulled = pulled + lax.dot_general(coupled, solved_lo, contract, preferred_element_type=jnp.float32)
    schur = boundary.astype(jnp.float32) - pulled
    if picks != owners:
        schur_hi, schur_lo = split_bf16(schur)
        schur = moved(schur_hi) + moved(schur_lo)
    return schur.reshape(owners, block_nodes, nodes)


def chain_weights(precond_f, couple_f):
    highest = lax.Precision.HIGHEST
    sections, block_nodes = precond_f.shape[0], precond_f.shape[1]
    step = jnp.einsum("gij,gjk->gik", precond_f, couple_f, precision=highest)
    eye = jnp.eye(block_nodes, dtype=jnp.float32)
    zero = jnp.zeros_like(eye)
    rows = []
    for h in range(sections):
        if h == 0:
            row = [eye] + [zero] * (sections - 1)
        else:
            row = [-jnp.dot(step[h], rows[h - 1][k], precision=highest) for k in range(h)]
            row = row + [eye] + [zero] * (sections - 1 - h)
        rows.append(row)
    return jnp.stack([jnp.stack(row) for row in rows])


def body(
    previous, right_side, precond, couple, block_ids, iface_matrix, interior_coupling, inv_interior
):
    high = lax.Precision.HIGH
    section_pos = lax.axis_index("section")
    sections = lax.axis_size("section")
    owners = lax.axis_size(OWNERS)
    block_nodes = previous.shape[1]
    load_count = previous.shape[2]
    nodes = owners * block_nodes

    tables = jnp.concatenate(
        [previous[0], precond[0, 0].astype(jnp.float32), couple[0, 0].astype(jnp.float32)],
        axis=1,
    )
    first_rounded = gather_owners(previous[0].astype(jnp.bfloat16))
    first_rounded, tables = lax.optimization_barrier((first_rounded, tables))
    tables = gather_along(tables, "section")
    start_all = tables[:, :, :load_count]
    precond_all = tables[:, :, load_count : load_count + block_nodes]
    couple_all = tables[:, :, load_count + block_nodes :]
    weights = chain_weights(precond_all, couple_all)
    above_pos = jnp.minimum(section_pos + 1, sections - 1)
    has_above = section_pos + 1 < sections
    behind = (section_pos - jnp.arange(sections)) % sections
    weights_mine = jnp.take(weights[section_pos], behind, axis=0)
    weights_above = jnp.take(weights[above_pos], behind, axis=0)
    precond_mine = precond[0, 0].astype(jnp.float32)
    couple_above = couple_all[above_pos]

    spread = schur_rows(
        block_ids[0, 0], iface_matrix[0, 0], interior_coupling[0, 0], inv_interior[0, 0], owners
    )
    tables, spread = lax.optimization_barrier((tables, spread))
    rows = jnp.sum(lax.all_to_all(spread, OWNERS, 0, 0, tiled=True), axis=0)
    rows = jnp.take(rows.reshape(block_nodes, owners, block_nodes), ring_owner_order(), axis=1)
    rows = rows.reshape(block_nodes, nodes)
    rows_hi, rows_lo = split_bf16(jnp.dot(precond_mine, rows, precision=lax.Precision.HIGHEST))

    temps_mine = previous[0]
    temps_above = start_all[above_pos]
    rhs = right_side[0]
    for sweep_index in range(SWEEPS):
        if sweep_index == 0:
            rounded = first_rounded
        else:
            rounded = gather_owners(temps_mine.astype(jnp.bfloat16))
        rounded = rounded.reshape(nodes, load_count)
        from_above = jnp.einsum("ij,il->jl", couple_above, temps_above, precision=high)
        from_above = jnp.where(has_above, from_above, 0.0)
        known = temps_mine + jnp.dot(precond_mine, rhs - from_above, precision=high)
        update = known - (
            jnp.dot(rows_hi, rounded, preferred_element_type=jnp.float32)
            + jnp.dot(rows_lo, rounded, preferred_element_type=jnp.float32)
        )
        updates = ring_parts(update, "section")
        temps_mine = jnp.einsum("kij,kjl->il", weights_mine, updates, precision=high)
        temps_above = jnp.einsum("kij,kjl->il", weights_above, updates, precision=high)
    return temps_mine[None]


def solution(mesh):
    in_specs = (
        P("section", OWNERS, None),
        P("section", OWNERS, None),
        P("section", OWNERS, None, None),
        P("section", OWNERS, None, None),
        P("section", OWNERS, None),
        P("section", OWNERS, None, None),
        P("section", OWNERS, None, None),
        P("section", OWNERS, None, None),
    )
    out_specs = P("section", OWNERS, None)
    return jax.shard_map(body, mesh=mesh, in_specs=in_specs, out_specs=out_specs, check_vma=False)
```

```python
import jax
import jax.numpy as jnp
from jax import lax
from jax.sharding import PartitionSpec as P

SWEEPS = 4
OWNERS = ("sub", "iface")


def split_bf16(value):
    high = lax.reduce_precision(value, exponent_bits=8, mantissa_bits=7)
    return high.astype(jnp.bfloat16), (value - high).astype(jnp.bfloat16)


def ring_parts(block, axis):
    count = lax.axis_size(axis)
    parts = [block]
    for distance in range(1, count):
        route = [(i, (i + distance) % count) for i in range(count)]
        parts.append(lax.ppermute(block, axis, route))
    return jnp.stack(parts)


def gather_owners(block):
    inner = ring_parts(block, "iface")
    outer = ring_parts(inner, "sub")
    return outer.reshape((-1,) + block.shape)


def ring_owner_order():
    subs, ifaces = lax.axis_size("sub"), lax.axis_size("iface")
    sub_back = (lax.axis_index("sub") - jnp.arange(subs)[:, None]) % subs
    iface_back = (lax.axis_index("iface") - jnp.arange(ifaces)[None, :]) % ifaces
    return (sub_back * ifaces + iface_back).reshape(-1)


def schur_rows(block_list, boundary, coupled, inverse, owners):
    picks = block_list.shape[0]
    block_nodes = boundary.shape[0] // picks
    nodes = owners * block_nodes
    contract = (((0,), (0,)), ((), ()))
    node = jnp.arange(nodes, dtype=jnp.int32)
    slot_node = jnp.arange(picks * block_nodes, dtype=jnp.int32)
    target = jnp.repeat(block_list, block_nodes) * block_nodes + slot_node % block_nodes
    place = (target[:, None] == node[None, :]).astype(jnp.bfloat16)

    def moved(matrix):
        rows = lax.dot_general(place, matrix, contract, preferred_element_type=jnp.float32)
        return jnp.dot(rows.astype(jnp.bfloat16), place, preferred_element_type=jnp.float32)

    if picks == owners:
        coupled = jnp.dot(coupled, place, preferred_element_type=jnp.float32).astype(jnp.bfloat16)
        boundary = moved(boundary)
    solved = jnp.dot(inverse, coupled, preferred_element_type=jnp.float32)
    solved_hi, solved_lo = split_bf16(solved)
    pulled = lax.dot_general(coupled, solved_hi, contract, preferred_element_type=jnp.float32)
    pulled = pulled + lax.dot_general(coupled, solved_lo, contract, preferred_element_type=jnp.float32)
    schur = boundary.astype(jnp.float32) - pulled
    if picks != owners:
        schur_hi, schur_lo = split_bf16(schur)
        schur = moved(schur_hi) + moved(schur_lo)
    return schur.reshape(owners, block_nodes, nodes)


def chain_weights(precond_f, couple_f):
    highest = lax.Precision.HIGHEST
    sections, block_nodes = precond_f.shape[0], precond_f.shape[1]
    step = jnp.einsum("gij,gjk->gik", precond_f, couple_f, precision=highest)
    eye = jnp.eye(block_nodes, dtype=jnp.float32)
    zero = jnp.zeros_like(eye)
    rows = []
    for h in range(sections):
        if h == 0:
            row = [eye] + [zero] * (sections - 1)
        else:
            row = [-jnp.dot(step[h], rows[h - 1][k], precision=highest) for k in range(h)]
            row = row + [eye] + [zero] * (sections - 1 - h)
        rows.append(row)
    return jnp.stack([jnp.stack(row) for row in rows])


def body(
    previous, right_side, precond, couple, block_ids, iface_matrix, interior_coupling, inv_interior
):
    high = lax.Precision.HIGH
    section_pos = lax.axis_index("section")
    sections = lax.axis_size("section")
    owners = lax.axis_size(OWNERS)
    block_nodes = previous.shape[1]
    load_count = previous.shape[2]
    nodes = owners * block_nodes

    tables = jnp.concatenate(
        [previous[0], precond[0, 0].astype(jnp.float32), couple[0, 0].astype(jnp.float32)],
        axis=1,
    )
    first_rounded = gather_owners(previous[0].astype(jnp.bfloat16))
    behind = (section_pos - jnp.arange(sections)) % sections
    tables = jnp.take(ring_parts(tables, "section"), behind, axis=0)
    start_all = tables[:, :, :load_count]
    precond_all = tables[:, :, load_count : load_count + block_nodes]
    couple_all = tables[:, :, load_count + block_nodes :]
    weights = chain_weights(precond_all, couple_all)
    above_pos = jnp.minimum(section_pos + 1, sections - 1)
    has_above = section_pos + 1 < sections
    weights_mine = jnp.take(weights[section_pos], behind, axis=0)
    weights_above = jnp.take(weights[above_pos], behind, axis=0)
    precond_mine = precond[0, 0].astype(jnp.float32)
    couple_above = couple_all[above_pos]

    spread = schur_rows(
        block_ids[0, 0], iface_matrix[0, 0], interior_coupling[0, 0], inv_interior[0, 0], owners
    )
    first_rounded, tables, spread = lax.optimization_barrier((first_rounded, tables, spread))
    rows = jnp.sum(lax.all_to_all(spread, OWNERS, 0, 0, tiled=True), axis=0)
    rows_hi, rows_lo = split_bf16(jnp.dot(precond_mine, rows, precision=lax.Precision.HIGHEST))
    node = jnp.arange(nodes, dtype=jnp.int32)
    source = jnp.repeat(ring_owner_order(), block_nodes) * block_nodes + node % block_nodes
    order = (node[:, None] == source[None, :]).astype(jnp.bfloat16)
    rows_hi = jnp.dot(rows_hi, order, preferred_element_type=jnp.float32).astype(jnp.bfloat16)
    rows_lo = jnp.dot(rows_lo, order, preferred_element_type=jnp.float32).astype(jnp.bfloat16)

    temps_mine = previous[0]
    temps_above = start_all[above_pos]
    rhs = right_side[0]
    for sweep_index in range(SWEEPS):
        if sweep_index == 0:
            rounded = first_rounded
        else:
            rounded = gather_owners(temps_mine.astype(jnp.bfloat16))
        rounded = rounded.reshape(nodes, load_count)
        from_above = jnp.einsum("ij,il->jl", couple_above, temps_above, precision=high)
        from_above = jnp.where(has_above, from_above, 0.0)
        known = temps_mine + jnp.dot(precond_mine, rhs - from_above, precision=high)
        update = known - (
            jnp.dot(rows_hi, rounded, preferred_element_type=jnp.float32)
            + jnp.dot(rows_lo, rounded, preferred_element_type=jnp.float32)
        )
        updates = ring_parts(update, "section")
        temps_mine = jnp.einsum("kij,kjl->il", weights_mine, updates, precision=high)
        temps_above = jnp.einsum("kij,kjl->il", weights_above, updates, precision=high)
    return temps_mine[None]


def solution(mesh):
    in_specs = (
        P("section", OWNERS, None),
        P("section", OWNERS, None),
        P("section", OWNERS, None, None),
        P("section", OWNERS, None, None),
        P("section", OWNERS, None),
        P("section", OWNERS, None, None),
        P("section", OWNERS, None, None),
        P("section", OWNERS, None, None),
    )
    out_specs = P("section", OWNERS, None)
    return jax.shard_map(body, mesh=mesh, in_specs=in_specs, out_specs=out_specs, check_vma=False)
```

```python
import jax
import jax.numpy as jnp
from jax import lax
from jax.sharding import PartitionSpec as P

SWEEPS = 4
OWNERS = ("sub", "iface")


def split_bf16(value):
    high = lax.reduce_precision(value, exponent_bits=8, mantissa_bits=7)
    return high.astype(jnp.bfloat16), (value - high).astype(jnp.bfloat16)


def ring_parts(block, axis):
    count = lax.axis_size(axis)
    parts = [block]
    for distance in range(1, count):
        route = [(i, (i + distance) % count) for i in range(count)]
        parts.append(lax.ppermute(block, axis, route))
    return jnp.stack(parts)


def gather_owners(block):
    inner = ring_parts(block, "iface")
    outer = ring_parts(inner, "sub")
    return outer.reshape((-1,) + block.shape)


def ring_owner_order():
    subs, ifaces = lax.axis_size("sub"), lax.axis_size("iface")
    sub_back = (lax.axis_index("sub") - jnp.arange(subs)[:, None]) % subs
    iface_back = (lax.axis_index("iface") - jnp.arange(ifaces)[None, :]) % ifaces
    return (sub_back * ifaces + iface_back).reshape(-1)


def schur_rows(block_list, boundary, coupled, inverse, owners):
    picks = block_list.shape[0]
    block_nodes = boundary.shape[0] // picks
    nodes = owners * block_nodes
    contract = (((0,), (0,)), ((), ()))
    node = jnp.arange(nodes, dtype=jnp.int32)
    slot_node = jnp.arange(picks * block_nodes, dtype=jnp.int32)
    target = jnp.repeat(block_list, block_nodes) * block_nodes + slot_node % block_nodes
    place = (target[:, None] == node[None, :]).astype(jnp.bfloat16)

    def moved(matrix):
        rows = lax.dot_general(place, matrix, contract, preferred_element_type=jnp.float32)
        return jnp.dot(rows.astype(jnp.bfloat16), place, preferred_element_type=jnp.float32)

    if picks == owners:
        coupled = jnp.dot(coupled, place, preferred_element_type=jnp.float32).astype(jnp.bfloat16)
        boundary = moved(boundary)
    solved = jnp.dot(inverse, coupled, preferred_element_type=jnp.float32)
    solved_hi, solved_lo = split_bf16(solved)
    pulled = lax.dot_general(coupled, solved_hi, contract, preferred_element_type=jnp.float32)
    pulled = pulled + lax.dot_general(coupled, solved_lo, contract, preferred_element_type=jnp.float32)
    schur = boundary.astype(jnp.float32) - pulled
    if picks != owners:
        schur_hi, schur_lo = split_bf16(schur)
        schur = moved(schur_hi) + moved(schur_lo)
    return schur.reshape(owners, block_nodes, nodes)


def chain_weights(precond_f, couple_f):
    highest = lax.Precision.HIGHEST
    sections, block_nodes = precond_f.shape[0], precond_f.shape[1]
    step = jnp.einsum("gij,gjk->gik", precond_f, couple_f, precision=highest)
    eye = jnp.eye(block_nodes, dtype=jnp.float32)
    zero = jnp.zeros_like(eye)
    rows = []
    for h in range(sections):
        if h == 0:
            row = [eye] + [zero] * (sections - 1)
        else:
            row = [-jnp.dot(step[h], rows[h - 1][k], precision=highest) for k in range(h)]
            row = row + [eye] + [zero] * (sections - 1 - h)
        rows.append(row)
    return jnp.stack([jnp.stack(row) for row in rows])


def body(
    previous, right_side, precond, couple, block_ids, iface_matrix, interior_coupling, inv_interior
):
    high = lax.Precision.HIGH
    section_pos = lax.axis_index("section")
    sections = lax.axis_size("section")
    owners = lax.axis_size(OWNERS)
    block_nodes = previous.shape[1]
    load_count = previous.shape[2]
    nodes = owners * block_nodes

    tables = jnp.concatenate(
        [previous[0], precond[0, 0].astype(jnp.float32), couple[0, 0].astype(jnp.float32)],
        axis=1,
    )
    first_rounded = gather_owners(previous[0].astype(jnp.bfloat16))
    behind = (section_pos - jnp.arange(sections)) % sections
    tables = jnp.take(ring_parts(tables, "section"), behind, axis=0)
    start_all = tables[:, :, :load_count]
    precond_all = tables[:, :, load_count : load_count + block_nodes]
    couple_all = tables[:, :, load_count + block_nodes :]
    weights = chain_weights(precond_all, couple_all)
    above_pos = jnp.minimum(section_pos + 1, sections - 1)
    has_above = section_pos + 1 < sections
    weights_mine = jnp.take(weights[section_pos], behind, axis=0)
    weights_above = jnp.take(weights[above_pos], behind, axis=0)
    precond_mine = precond[0, 0].astype(jnp.float32)
    couple_above = couple_all[above_pos]

    spread = schur_rows(
        block_ids[0, 0], iface_matrix[0, 0], interior_coupling[0, 0], inv_interior[0, 0], owners
    )
    temps_mine = previous[0]
    temps_above = start_all[above_pos]
    rhs = right_side[0]

    def known_part(temps_mine, temps_above):
        from_above = jnp.einsum("ij,il->jl", couple_above, temps_above, precision=high)
        from_above = jnp.where(has_above, from_above, 0.0)
        return temps_mine + jnp.dot(precond_mine, rhs - from_above, precision=high)

    known = known_part(temps_mine, temps_above)
    first_rounded, weights_mine, weights_above, known, spread = lax.optimization_barrier(
        (first_rounded, weights_mine, weights_above, known, spread)
    )
    rows = jnp.sum(lax.all_to_all(spread, OWNERS, 0, 0, tiled=True), axis=0)
    rows_hi, rows_lo = split_bf16(jnp.dot(precond_mine, rows, precision=lax.Precision.HIGHEST))
    node = jnp.arange(nodes, dtype=jnp.int32)
    source = jnp.repeat(ring_owner_order(), block_nodes) * block_nodes + node % block_nodes
    order = (node[:, None] == source[None, :]).astype(jnp.bfloat16)
    rows_hi = jnp.dot(rows_hi, order, preferred_element_type=jnp.float32).astype(jnp.bfloat16)
    rows_lo = jnp.dot(rows_lo, order, preferred_element_type=jnp.float32).astype(jnp.bfloat16)

    for sweep_index in range(SWEEPS):
        if sweep_index == 0:
            rounded = first_rounded
        else:
            rounded = gather_owners(temps_mine.astype(jnp.bfloat16))
            known = known_part(temps_mine, temps_above)
        rounded = rounded.reshape(nodes, load_count)
        update = known - (
            jnp.dot(rows_hi, rounded, preferred_element_type=jnp.float32)
            + jnp.dot(rows_lo, rounded, preferred_element_type=jnp.float32)
        )
        updates = ring_parts(update, "section")
        temps_mine = jnp.einsum("kij,kjl->il", weights_mine, updates, precision=high)
        temps_above = jnp.einsum("kij,kjl->il", weights_above, updates, precision=high)
    return temps_mine[None]


def solution(mesh):
    in_specs = (
        P("section", OWNERS, None),
        P("section", OWNERS, None),
        P("section", OWNERS, None, None),
        P("section", OWNERS, None, None),
        P("section", OWNERS, None),
        P("section", OWNERS, None, None),
        P("section", OWNERS, None, None),
        P("section", OWNERS, None, None),
    )
    out_specs = P("section", OWNERS, None)
    return jax.shard_map(body, mesh=mesh, in_specs=in_specs, out_specs=out_specs, check_vma=False)
```

```python
import jax
import jax.numpy as jnp
from jax import lax
from jax.sharding import PartitionSpec as P

SWEEPS = 4
OWNERS = ("sub", "iface")


def split_bf16(value):
    high = lax.reduce_precision(value, exponent_bits=8, mantissa_bits=7)
    return high.astype(jnp.bfloat16), (value - high).astype(jnp.bfloat16)


def ring_parts(block, axis):
    count = lax.axis_size(axis)
    parts = [block]
    for distance in range(1, count):
        route = [(i, (i + distance) % count) for i in range(count)]
        parts.append(lax.ppermute(block, axis, route))
    return jnp.stack(parts)


def gather_owners(block):
    inner = ring_parts(block, "iface")
    outer = ring_parts(inner, "sub")
    return outer.reshape((-1,) + block.shape)


def ring_owner_order():
    subs, ifaces = lax.axis_size("sub"), lax.axis_size("iface")
    sub_back = (lax.axis_index("sub") - jnp.arange(subs)[:, None]) % subs
    iface_back = (lax.axis_index("iface") - jnp.arange(ifaces)[None, :]) % ifaces
    return (sub_back * ifaces + iface_back).reshape(-1)


def scatter_owners(terms):
    subs, ifaces = lax.axis_size("sub"), lax.axis_size("iface")
    sub_pos, iface_pos = lax.axis_index("sub"), lax.axis_index("iface")
    terms = terms.reshape((subs, ifaces) + terms.shape[1:])
    inner = lax.dynamic_index_in_dim(terms, iface_pos, axis=1, keepdims=False)
    for distance in range(1, ifaces):
        route = [(i, (i + distance) % ifaces) for i in range(ifaces)]
        chunk = lax.dynamic_index_in_dim(terms, (iface_pos + distance) % ifaces, axis=1, keepdims=False)
        inner = inner + lax.ppermute(chunk, "iface", route)
    total = lax.dynamic_index_in_dim(inner, sub_pos, axis=0, keepdims=False)
    for distance in range(1, subs):
        route = [(i, (i + distance) % subs) for i in range(subs)]
        chunk = lax.dynamic_index_in_dim(inner, (sub_pos + distance) % subs, axis=0, keepdims=False)
        total = total + lax.ppermute(chunk, "sub", route)
    return total


def schur_rows(block_list, boundary, coupled, inverse, owners):
    picks = block_list.shape[0]
    block_nodes = boundary.shape[0] // picks
    nodes = owners * block_nodes
    contract = (((0,), (0,)), ((), ()))
    node = jnp.arange(nodes, dtype=jnp.int32)
    slot_node = jnp.arange(picks * block_nodes, dtype=jnp.int32)
    target = jnp.repeat(block_list, block_nodes) * block_nodes + slot_node % block_nodes
    place = (target[:, None] == node[None, :]).astype(jnp.bfloat16)

    def moved(matrix):
        rows = lax.dot_general(place, matrix, contract, preferred_element_type=jnp.float32)
        return jnp.dot(rows.astype(jnp.bfloat16), place, preferred_element_type=jnp.float32)

    if picks == owners:
        coupled = jnp.dot(coupled, place, preferred_element_type=jnp.float32).astype(jnp.bfloat16)
        boundary = moved(boundary)
    solved = jnp.dot(inverse, coupled, preferred_element_type=jnp.float32)
    solved_hi, solved_lo = split_bf16(solved)
    pulled = lax.dot_general(coupled, solved_hi, contract, preferred_element_type=jnp.float32)
    pulled = pulled + lax.dot_general(coupled, solved_lo, contract, preferred_element_type=jnp.float32)
    schur = boundary.astype(jnp.float32) - pulled
    if picks != owners:
        schur_hi, schur_lo = split_bf16(schur)
        schur = moved(schur_hi) + moved(schur_lo)
    return schur.reshape(owners, block_nodes, nodes)


def chain_weights(precond_f, couple_f):
    highest = lax.Precision.HIGHEST
    sections, block_nodes = precond_f.shape[0], precond_f.shape[1]
    step = jnp.einsum("gij,gjk->gik", precond_f, couple_f, precision=highest)
    eye = jnp.eye(block_nodes, dtype=jnp.float32)
    zero = jnp.zeros_like(eye)
    rows = []
    for h in range(sections):
        if h == 0:
            row = [eye] + [zero] * (sections - 1)
        else:
            row = [-jnp.dot(step[h], rows[h - 1][k], precision=highest) for k in range(h)]
            row = row + [eye] + [zero] * (sections - 1 - h)
        rows.append(row)
    return jnp.stack([jnp.stack(row) for row in rows])


def body(
    previous, right_side, precond, couple, block_ids, iface_matrix, interior_coupling, inv_interior
):
    high = lax.Precision.HIGH
    section_pos = lax.axis_index("section")
    sections = lax.axis_size("section")
    owners = lax.axis_size(OWNERS)
    block_nodes = previous.shape[1]
    load_count = previous.shape[2]
    nodes = owners * block_nodes

    tables = jnp.concatenate(
        [previous[0], precond[0, 0].astype(jnp.float32), couple[0, 0].astype(jnp.float32)],
        axis=1,
    )
    first_rounded = gather_owners(previous[0].astype(jnp.bfloat16))
    behind = (section_pos - jnp.arange(sections)) % sections
    tables = jnp.take(ring_parts(tables, "section"), behind, axis=0)
    start_all = tables[:, :, :load_count]
    precond_all = tables[:, :, load_count : load_count + block_nodes]
    couple_all = tables[:, :, load_count + block_nodes :]
    weights = chain_weights(precond_all, couple_all)
    above_pos = jnp.minimum(section_pos + 1, sections - 1)
    has_above = section_pos + 1 < sections
    weights_mine = jnp.take(weights[section_pos], behind, axis=0)
    weights_above = jnp.take(weights[above_pos], behind, axis=0)
    precond_mine = precond[0, 0].astype(jnp.float32)
    couple_above = couple_all[above_pos]

    spread = schur_rows(
        block_ids[0, 0], iface_matrix[0, 0], interior_coupling[0, 0], inv_interior[0, 0], owners
    )
    temps_mine = previous[0]
    temps_above = start_all[above_pos]
    rhs = right_side[0]

    def known_part(temps_mine, temps_above):
        from_above = jnp.einsum("ij,il->jl", couple_above, temps_above, precision=high)
        from_above = jnp.where(has_above, from_above, 0.0)
        return temps_mine + jnp.dot(precond_mine, rhs - from_above, precision=high)

    known = known_part(temps_mine, temps_above)
    first_rounded, weights_mine, weights_above, known, spread = lax.optimization_barrier(
        (first_rounded, weights_mine, weights_above, known, spread)
    )
    node = jnp.arange(nodes, dtype=jnp.int32)
    source = jnp.repeat(ring_owner_order(), block_nodes) * block_nodes + node % block_nodes
    order = (node[:, None] == source[None, :]).astype(jnp.bfloat16)
    first_nodes = first_rounded.reshape(nodes, load_count)
    first_nodes = jnp.dot(order, first_nodes, preferred_element_type=jnp.float32).astype(jnp.bfloat16)
    schur_hi, schur_lo = split_bf16(spread.reshape(nodes, nodes))
    first_terms = jnp.dot(schur_hi, first_nodes, preferred_element_type=jnp.float32) + jnp.dot(
        schur_lo, first_nodes, preferred_element_type=jnp.float32
    )
    first_assembled = scatter_owners(first_terms.reshape(owners, block_nodes, load_count))
    rows = jnp.sum(lax.all_to_all(spread, OWNERS, 0, 0, tiled=True), axis=0)
    rows_hi, rows_lo = split_bf16(jnp.dot(precond_mine, rows, precision=lax.Precision.HIGHEST))
    rows_hi = jnp.dot(rows_hi, order, preferred_element_type=jnp.float32).astype(jnp.bfloat16)
    rows_lo = jnp.dot(rows_lo, order, preferred_element_type=jnp.float32).astype(jnp.bfloat16)

    for sweep_index in range(SWEEPS):
        if sweep_index == 0:
            update = known - jnp.dot(precond_mine, first_assembled, precision=high)
        else:
            rounded = gather_owners(temps_mine.astype(jnp.bfloat16)).reshape(nodes, load_count)
            known = known_part(temps_mine, temps_above)
            update = known - (
                jnp.dot(rows_hi, rounded, preferred_element_type=jnp.float32)
                + jnp.dot(rows_lo, rounded, preferred_element_type=jnp.float32)
            )
        updates = ring_parts(update, "section")
        temps_mine = jnp.einsum("kij,kjl->il", weights_mine, updates, precision=high)
        temps_above = jnp.einsum("kij,kjl->il", weights_above, updates, precision=high)
    return temps_mine[None]


def solution(mesh):
    in_specs = (
        P("section", OWNERS, None),
        P("section", OWNERS, None),
        P("section", OWNERS, None, None),
        P("section", OWNERS, None, None),
        P("section", OWNERS, None),
        P("section", OWNERS, None, None),
        P("section", OWNERS, None, None),
        P("section", OWNERS, None, None),
    )
    out_specs = P("section", OWNERS, None)
    return jax.shard_map(body, mesh=mesh, in_specs=in_specs, out_specs=out_specs, check_vma=False)
```

```python
import jax
import jax.numpy as jnp
from jax import lax
from jax.sharding import PartitionSpec as P

SWEEPS = 4
OWNERS = ("sub", "iface")


def split_bf16(value):
    high = lax.reduce_precision(value, exponent_bits=8, mantissa_bits=7)
    return high.astype(jnp.bfloat16), (value - high).astype(jnp.bfloat16)


def swap_parts(block, axis):
    count = lax.axis_size(axis)
    parts = block[None]
    bit = 1
    while bit < count:
        route = [(i, i ^ bit) for i in range(count)]
        parts = jnp.concatenate([parts, lax.ppermute(parts, axis, route)], axis=0)
        bit *= 2
    return parts


def gather_owners(block):
    return swap_parts(block, OWNERS)


def partner_order(axis):
    return lax.axis_index(axis) ^ jnp.arange(lax.axis_size(axis))


def schur_rows(block_list, boundary, coupled, inverse, owners):
    picks = block_list.shape[0]
    block_nodes = boundary.shape[0] // picks
    nodes = owners * block_nodes
    contract = (((0,), (0,)), ((), ()))
    node = jnp.arange(nodes, dtype=jnp.int32)
    slot_node = jnp.arange(picks * block_nodes, dtype=jnp.int32)
    target = jnp.repeat(block_list, block_nodes) * block_nodes + slot_node % block_nodes
    place = (target[:, None] == node[None, :]).astype(jnp.bfloat16)

    def moved(matrix):
        rows = lax.dot_general(place, matrix, contract, preferred_element_type=jnp.float32)
        return jnp.dot(rows.astype(jnp.bfloat16), place, preferred_element_type=jnp.float32)

    if picks == owners:
        coupled = jnp.dot(coupled, place, preferred_element_type=jnp.float32).astype(jnp.bfloat16)
        boundary = moved(boundary)
    solved = jnp.dot(inverse, coupled, preferred_element_type=jnp.float32)
    solved_hi, solved_lo = split_bf16(solved)
    pulled = lax.dot_general(coupled, solved_hi, contract, preferred_element_type=jnp.float32)
    pulled = pulled + lax.dot_general(coupled, solved_lo, contract, preferred_element_type=jnp.float32)
    schur = boundary.astype(jnp.float32) - pulled
    if picks != owners:
        schur_hi, schur_lo = split_bf16(schur)
        schur = moved(schur_hi) + moved(schur_lo)
    return schur.reshape(owners, block_nodes, nodes)


def chain_weights(precond_f, couple_f):
    highest = lax.Precision.HIGHEST
    sections, block_nodes = precond_f.shape[0], precond_f.shape[1]
    step = jnp.einsum("gij,gjk->gik", precond_f, couple_f, precision=highest)
    eye = jnp.eye(block_nodes, dtype=jnp.float32)
    zero = jnp.zeros_like(eye)
    rows = []
    for h in range(sections):
        if h == 0:
            row = [eye] + [zero] * (sections - 1)
        else:
            row = [-jnp.dot(step[h], rows[h - 1][k], precision=highest) for k in range(h)]
            row = row + [eye] + [zero] * (sections - 1 - h)
        rows.append(row)
    return jnp.stack([jnp.stack(row) for row in rows])


def body(
    previous, right_side, precond, couple, block_ids, iface_matrix, interior_coupling, inv_interior
):
    high = lax.Precision.HIGH
    section_pos = lax.axis_index("section")
    sections = lax.axis_size("section")
    owners = lax.axis_size(OWNERS)
    block_nodes = previous.shape[1]
    load_count = previous.shape[2]
    nodes = owners * block_nodes

    tables = jnp.concatenate(
        [previous[0], precond[0, 0].astype(jnp.float32), couple[0, 0].astype(jnp.float32)],
        axis=1,
    )
    first_rounded = gather_owners(previous[0].astype(jnp.bfloat16))
    behind = partner_order("section")
    tables = jnp.take(swap_parts(tables, "section"), behind, axis=0)
    start_all = tables[:, :, :load_count]
    precond_all = tables[:, :, load_count : load_count + block_nodes]
    couple_all = tables[:, :, load_count + block_nodes :]
    weights = chain_weights(precond_all, couple_all)
    above_pos = jnp.minimum(section_pos + 1, sections - 1)
    has_above = section_pos + 1 < sections
    weights_mine = jnp.take(weights[section_pos], behind, axis=0)
    weights_above = jnp.take(weights[above_pos], behind, axis=0)
    precond_mine = precond[0, 0].astype(jnp.float32)
    couple_above = couple_all[above_pos]

    spread = schur_rows(
        block_ids[0, 0], iface_matrix[0, 0], interior_coupling[0, 0], inv_interior[0, 0], owners
    )
    temps_mine = previous[0]
    temps_above = start_all[above_pos]
    rhs = right_side[0]

    def known_part(temps_mine, temps_above):
        from_above = jnp.einsum("ij,il->jl", couple_above, temps_above, precision=high)
        from_above = jnp.where(has_above, from_above, 0.0)
        return temps_mine + jnp.dot(precond_mine, rhs - from_above, precision=high)

    known = known_part(temps_mine, temps_above)
    first_rounded, weights_mine, weights_above, known, spread = lax.optimization_barrier(
        (first_rounded, weights_mine, weights_above, known, spread)
    )
    rows = jnp.sum(lax.all_to_all(spread, OWNERS, 0, 0, tiled=True), axis=0)
    rows_hi, rows_lo = split_bf16(jnp.dot(precond_mine, rows, precision=lax.Precision.HIGHEST))
    node = jnp.arange(nodes, dtype=jnp.int32)
    source = jnp.repeat(partner_order(OWNERS), block_nodes) * block_nodes + node % block_nodes
    order = (node[:, None] == source[None, :]).astype(jnp.bfloat16)
    rows_hi = jnp.dot(rows_hi, order, preferred_element_type=jnp.float32).astype(jnp.bfloat16)
    rows_lo = jnp.dot(rows_lo, order, preferred_element_type=jnp.float32).astype(jnp.bfloat16)

    for sweep_index in range(SWEEPS):
        if sweep_index == 0:
            rounded = first_rounded
        else:
            rounded = gather_owners(temps_mine.astype(jnp.bfloat16))
            known = known_part(temps_mine, temps_above)
        rounded = rounded.reshape(nodes, load_count)
        update = known - (
            jnp.dot(rows_hi, rounded, preferred_element_type=jnp.float32)
            + jnp.dot(rows_lo, rounded, preferred_element_type=jnp.float32)
        )
        updates = swap_parts(update, "section")
        temps_mine = jnp.einsum("kij,kjl->il", weights_mine, updates, precision=high)
        temps_above = jnp.einsum("kij,kjl->il", weights_above, updates, precision=high)
    return temps_mine[None]


def solution(mesh):
    in_specs = (
        P("section", OWNERS, None),
        P("section", OWNERS, None),
        P("section", OWNERS, None, None),
        P("section", OWNERS, None, None),
        P("section", OWNERS, None),
        P("section", OWNERS, None, None),
        P("section", OWNERS, None, None),
        P("section", OWNERS, None, None),
    )
    out_specs = P("section", OWNERS, None)
    return jax.shard_map(body, mesh=mesh, in_specs=in_specs, out_specs=out_specs, check_vma=False)
```

```python
import jax
import jax.numpy as jnp
from jax import lax
from jax.sharding import PartitionSpec as P

SWEEPS = 4
OWNERS = ("sub", "iface")


def split_bf16(value):
    high = lax.reduce_precision(value, exponent_bits=8, mantissa_bits=7)
    return high.astype(jnp.bfloat16), (value - high).astype(jnp.bfloat16)


def ring_parts(block, axis):
    count = lax.axis_size(axis)
    parts = [block]
    for distance in range(1, count):
        route = [(i, (i + distance) % count) for i in range(count)]
        parts.append(lax.ppermute(block, axis, route))
    return jnp.stack(parts)


def gather_owners(block):
    subs, ifaces = lax.axis_size("sub"), lax.axis_size("iface")
    parts = []
    for sub_step in range(subs):
        for iface_step in range(ifaces):
            if sub_step == 0 and iface_step == 0:
                parts.append(block)
                continue
            route = [
                (s * ifaces + i, ((s + sub_step) % subs) * ifaces + (i + iface_step) % ifaces)
                for s in range(subs)
                for i in range(ifaces)
            ]
            parts.append(lax.ppermute(block, OWNERS, route))
    return jnp.stack(parts)


def ring_owner_order():
    subs, ifaces = lax.axis_size("sub"), lax.axis_size("iface")
    sub_back = (lax.axis_index("sub") - jnp.arange(subs)[:, None]) % subs
    iface_back = (lax.axis_index("iface") - jnp.arange(ifaces)[None, :]) % ifaces
    return (sub_back * ifaces + iface_back).reshape(-1)


def schur_rows(block_list, boundary, coupled, inverse, owners):
    picks = block_list.shape[0]
    block_nodes = boundary.shape[0] // picks
    nodes = owners * block_nodes
    contract = (((0,), (0,)), ((), ()))
    node = jnp.arange(nodes, dtype=jnp.int32)
    slot_node = jnp.arange(picks * block_nodes, dtype=jnp.int32)
    target = jnp.repeat(block_list, block_nodes) * block_nodes + slot_node % block_nodes
    place = (target[:, None] == node[None, :]).astype(jnp.bfloat16)

    def moved(matrix):
        rows = lax.dot_general(place, matrix, contract, preferred_element_type=jnp.float32)
        return jnp.dot(rows.astype(jnp.bfloat16), place, preferred_element_type=jnp.float32)

    if picks == owners:
        coupled = jnp.dot(coupled, place, preferred_element_type=jnp.float32).astype(jnp.bfloat16)
        boundary = moved(boundary)
    solved = jnp.dot(inverse, coupled, preferred_element_type=jnp.float32)
    solved_hi, solved_lo = split_bf16(solved)
    pulled = lax.dot_general(coupled, solved_hi, contract, preferred_element_type=jnp.float32)
    pulled = pulled + lax.dot_general(coupled, solved_lo, contract, preferred_element_type=jnp.float32)
    schur = boundary.astype(jnp.float32) - pulled
    if picks != owners:
        schur_hi, schur_lo = split_bf16(schur)
        schur = moved(schur_hi) + moved(schur_lo)
    return schur.reshape(owners, block_nodes, nodes)


def chain_weights(precond_f, couple_f):
    highest = lax.Precision.HIGHEST
    sections, block_nodes = precond_f.shape[0], precond_f.shape[1]
    step = jnp.einsum("gij,gjk->gik", precond_f, couple_f, precision=highest)
    eye = jnp.eye(block_nodes, dtype=jnp.float32)
    zero = jnp.zeros_like(eye)
    rows = []
    for h in range(sections):
        if h == 0:
            row = [eye] + [zero] * (sections - 1)
        else:
            row = [-jnp.dot(step[h], rows[h - 1][k], precision=highest) for k in range(h)]
            row = row + [eye] + [zero] * (sections - 1 - h)
        rows.append(row)
    return jnp.stack([jnp.stack(row) for row in rows])


def body(
    previous, right_side, precond, couple, block_ids, iface_matrix, interior_coupling, inv_interior
):
    high = lax.Precision.HIGH
    section_pos = lax.axis_index("section")
    sections = lax.axis_size("section")
    owners = lax.axis_size(OWNERS)
    block_nodes = previous.shape[1]
    load_count = previous.shape[2]
    nodes = owners * block_nodes

    tables = jnp.concatenate(
        [previous[0], precond[0, 0].astype(jnp.float32), couple[0, 0].astype(jnp.float32)],
        axis=1,
    )
    first_rounded = gather_owners(previous[0].astype(jnp.bfloat16))
    behind = (section_pos - jnp.arange(sections)) % sections
    tables = jnp.take(ring_parts(tables, "section"), behind, axis=0)
    start_all = tables[:, :, :load_count]
    precond_all = tables[:, :, load_count : load_count + block_nodes]
    couple_all = tables[:, :, load_count + block_nodes :]
    weights = chain_weights(precond_all, couple_all)
    above_pos = jnp.minimum(section_pos + 1, sections - 1)
    has_above = section_pos + 1 < sections
    weights_mine = jnp.take(weights[section_pos], behind, axis=0)
    weights_above = jnp.take(weights[above_pos], behind, axis=0)
    precond_mine = precond[0, 0].astype(jnp.float32)
    couple_above = couple_all[above_pos]

    spread = schur_rows(
        block_ids[0, 0], iface_matrix[0, 0], interior_coupling[0, 0], inv_interior[0, 0], owners
    )
    temps_mine = previous[0]
    temps_above = start_all[above_pos]
    rhs = right_side[0]

    def known_part(temps_mine, temps_above):
        from_above = jnp.einsum("ij,il->jl", couple_above, temps_above, precision=high)
        from_above = jnp.where(has_above, from_above, 0.0)
        return temps_mine + jnp.dot(precond_mine, rhs - from_above, precision=high)

    known = known_part(temps_mine, temps_above)
    first_rounded, weights_mine, weights_above, known, spread = lax.optimization_barrier(
        (first_rounded, weights_mine, weights_above, known, spread)
    )
    rows = jnp.sum(lax.all_to_all(spread, OWNERS, 0, 0, tiled=True), axis=0)
    rows_hi, rows_lo = split_bf16(jnp.dot(precond_mine, rows, precision=lax.Precision.HIGHEST))
    node = jnp.arange(nodes, dtype=jnp.int32)
    source = jnp.repeat(ring_owner_order(), block_nodes) * block_nodes + node % block_nodes
    order = (node[:, None] == source[None, :]).astype(jnp.bfloat16)
    rows_hi = jnp.dot(rows_hi, order, preferred_element_type=jnp.float32).astype(jnp.bfloat16)
    rows_lo = jnp.dot(rows_lo, order, preferred_element_type=jnp.float32).astype(jnp.bfloat16)

    for sweep_index in range(SWEEPS):
        if sweep_index == 0:
            rounded = first_rounded
        else:
            rounded = gather_owners(temps_mine.astype(jnp.bfloat16))
            known = known_part(temps_mine, temps_above)
        rounded = rounded.reshape(nodes, load_count)
        update = known - (
            jnp.dot(rows_hi, rounded, preferred_element_type=jnp.float32)
            + jnp.dot(rows_lo, rounded, preferred_element_type=jnp.float32)
        )
        updates = ring_parts(update, "section")
        temps_mine = jnp.einsum("kij,kjl->il", weights_mine, updates, precision=high)
        temps_above = jnp.einsum("kij,kjl->il", weights_above, updates, precision=high)
    return temps_mine[None]


def solution(mesh):
    in_specs = (
        P("section", OWNERS, None),
        P("section", OWNERS, None),
        P("section", OWNERS, None, None),
        P("section", OWNERS, None, None),
        P("section", OWNERS, None),
        P("section", OWNERS, None, None),
        P("section", OWNERS, None, None),
        P("section", OWNERS, None, None),
    )
    out_specs = P("section", OWNERS, None)
    return jax.shard_map(body, mesh=mesh, in_specs=in_specs, out_specs=out_specs, check_vma=False)
```

```python
import jax
import jax.numpy as jnp
from jax import lax
from jax.sharding import PartitionSpec as P

SWEEPS = 4
OWNERS = ("sub", "iface")


def split_bf16(value):
    high = lax.reduce_precision(value, exponent_bits=8, mantissa_bits=7)
    return high.astype(jnp.bfloat16), (value - high).astype(jnp.bfloat16)


def ring_parts(block, axis):
    count = lax.axis_size(axis)
    parts = [block]
    for distance in range(1, count):
        route = [(i, (i + distance) % count) for i in range(count)]
        parts.append(lax.ppermute(block, axis, route))
    return jnp.stack(parts)


def gather_owners(block):
    inner = ring_parts(block, "iface")
    outer = ring_parts(inner, "sub")
    return outer.reshape((-1,) + block.shape)


def ring_owner_order():
    subs, ifaces = lax.axis_size("sub"), lax.axis_size("iface")
    sub_back = (lax.axis_index("sub") - jnp.arange(subs)[:, None]) % subs
    iface_back = (lax.axis_index("iface") - jnp.arange(ifaces)[None, :]) % ifaces
    return (sub_back * ifaces + iface_back).reshape(-1)


def scatter_owners(terms):
    subs, ifaces = lax.axis_size("sub"), lax.axis_size("iface")
    sub_pos, iface_pos = lax.axis_index("sub"), lax.axis_index("iface")
    terms = terms.reshape((subs, ifaces) + terms.shape[1:])
    inner = lax.dynamic_index_in_dim(terms, iface_pos, axis=1, keepdims=False)
    for distance in range(1, ifaces):
        route = [(i, (i + distance) % ifaces) for i in range(ifaces)]
        chunk = lax.dynamic_index_in_dim(terms, (iface_pos + distance) % ifaces, axis=1, keepdims=False)
        inner = inner + lax.ppermute(chunk, "iface", route)
    total = lax.dynamic_index_in_dim(inner, sub_pos, axis=0, keepdims=False)
    for distance in range(1, subs):
        route = [(i, (i + distance) % subs) for i in range(subs)]
        chunk = lax.dynamic_index_in_dim(inner, (sub_pos + distance) % subs, axis=0, keepdims=False)
        total = total + lax.ppermute(chunk, "sub", route)
    return total


def schur_rows(block_list, boundary, coupled, inverse, owners):
    picks = block_list.shape[0]
    block_nodes = boundary.shape[0] // picks
    nodes = owners * block_nodes
    contract = (((0,), (0,)), ((), ()))
    node = jnp.arange(nodes, dtype=jnp.int32)
    slot_node = jnp.arange(picks * block_nodes, dtype=jnp.int32)
    target = jnp.repeat(block_list, block_nodes) * block_nodes + slot_node % block_nodes
    place = (target[:, None] == node[None, :]).astype(jnp.bfloat16)

    def moved(matrix):
        rows = lax.dot_general(place, matrix, contract, preferred_element_type=jnp.float32)
        return jnp.dot(rows.astype(jnp.bfloat16), place, preferred_element_type=jnp.float32)

    if picks == owners:
        coupled = jnp.dot(coupled, place, preferred_element_type=jnp.float32).astype(jnp.bfloat16)
        boundary = moved(boundary)
    solved = jnp.dot(inverse, coupled, preferred_element_type=jnp.float32)
    solved_hi, solved_lo = split_bf16(solved)
    pulled = lax.dot_general(coupled, solved_hi, contract, preferred_element_type=jnp.float32)
    pulled = pulled + lax.dot_general(coupled, solved_lo, contract, preferred_element_type=jnp.float32)
    schur = boundary.astype(jnp.float32) - pulled
    if picks != owners:
        schur_hi, schur_lo = split_bf16(schur)
        schur = moved(schur_hi) + moved(schur_lo)
    return schur.reshape(owners, block_nodes, nodes)


def chain_weights(precond_f, couple_f):
    highest = lax.Precision.HIGHEST
    sections, block_nodes = precond_f.shape[0], precond_f.shape[1]
    step = jnp.einsum("gij,gjk->gik", precond_f, couple_f, precision=highest)
    eye = jnp.eye(block_nodes, dtype=jnp.float32)
    zero = jnp.zeros_like(eye)
    rows = []
    for h in range(sections):
        if h == 0:
            row = [eye] + [zero] * (sections - 1)
        else:
            row = [-jnp.dot(step[h], rows[h - 1][k], precision=highest) for k in range(h)]
            row = row + [eye] + [zero] * (sections - 1 - h)
        rows.append(row)
    return jnp.stack([jnp.stack(row) for row in rows])


def body(
    previous, right_side, precond, couple, block_ids, iface_matrix, interior_coupling, inv_interior
):
    high = lax.Precision.HIGH
    section_pos = lax.axis_index("section")
    sections = lax.axis_size("section")
    owners = lax.axis_size(OWNERS)
    block_nodes = previous.shape[1]
    load_count = previous.shape[2]
    nodes = owners * block_nodes

    tables = jnp.concatenate(
        [previous[0], precond[0, 0].astype(jnp.float32), couple[0, 0].astype(jnp.float32)],
        axis=1,
    )
    first_rounded = gather_owners(previous[0].astype(jnp.bfloat16))
    behind = (section_pos - jnp.arange(sections)) % sections
    tables = jnp.take(ring_parts(tables, "section"), behind, axis=0)
    start_all = tables[:, :, :load_count]
    precond_all = tables[:, :, load_count : load_count + block_nodes]
    couple_all = tables[:, :, load_count + block_nodes :]
    weights = chain_weights(precond_all, couple_all)
    above_pos = jnp.minimum(section_pos + 1, sections - 1)
    has_above = section_pos + 1 < sections
    weights_mine = jnp.take(weights[section_pos], behind, axis=0)
    weights_above = jnp.take(weights[above_pos], behind, axis=0)
    precond_mine = precond[0, 0].astype(jnp.float32)
    couple_above = couple_all[above_pos]

    spread = schur_rows(
        block_ids[0, 0], iface_matrix[0, 0], interior_coupling[0, 0], inv_interior[0, 0], owners
    )
    temps_mine = previous[0]
    temps_above = start_all[above_pos]
    rhs = right_side[0]

    def known_part(temps_mine, temps_above):
        from_above = jnp.einsum("ij,il->jl", couple_above, temps_above, precision=high)
        from_above = jnp.where(has_above, from_above, 0.0)
        return temps_mine + jnp.dot(precond_mine, rhs - from_above, precision=high)

    known = known_part(temps_mine, temps_above)
    first_rounded, weights_mine, weights_above, known, spread = lax.optimization_barrier(
        (first_rounded, weights_mine, weights_above, known, spread)
    )
    rows = scatter_owners(spread)
    rows_hi, rows_lo = split_bf16(jnp.dot(precond_mine, rows, precision=lax.Precision.HIGHEST))
    node = jnp.arange(nodes, dtype=jnp.int32)
    source = jnp.repeat(ring_owner_order(), block_nodes) * block_nodes + node % block_nodes
    order = (node[:, None] == source[None, :]).astype(jnp.bfloat16)
    rows_hi = jnp.dot(rows_hi, order, preferred_element_type=jnp.float32).astype(jnp.bfloat16)
    rows_lo = jnp.dot(rows_lo, order, preferred_element_type=jnp.float32).astype(jnp.bfloat16)

    for sweep_index in range(SWEEPS):
        if sweep_index == 0:
            rounded = first_rounded
        else:
            rounded = gather_owners(temps_mine.astype(jnp.bfloat16))
            known = known_part(temps_mine, temps_above)
        rounded = rounded.reshape(nodes, load_count)
        update = known - (
            jnp.dot(rows_hi, rounded, preferred_element_type=jnp.float32)
            + jnp.dot(rows_lo, rounded, preferred_element_type=jnp.float32)
        )
        updates = ring_parts(update, "section")
        temps_mine = jnp.einsum("kij,kjl->il", weights_mine, updates, precision=high)
        temps_above = jnp.einsum("kij,kjl->il", weights_above, updates, precision=high)
    return temps_mine[None]


def solution(mesh):
    in_specs = (
        P("section", OWNERS, None),
        P("section", OWNERS, None),
        P("section", OWNERS, None, None),
        P("section", OWNERS, None, None),
        P("section", OWNERS, None),
        P("section", OWNERS, None, None),
        P("section", OWNERS, None, None),
        P("section", OWNERS, None, None),
    )
    out_specs = P("section", OWNERS, None)
    return jax.shard_map(body, mesh=mesh, in_specs=in_specs, out_specs=out_specs, check_vma=False)
```

```python
import jax
import jax.numpy as jnp
from jax import lax
from jax.sharding import PartitionSpec as P

SWEEPS = 4
OWNERS = ("sub", "iface")


def split_bf16(value):
    high = lax.reduce_precision(value, exponent_bits=8, mantissa_bits=7)
    return high.astype(jnp.bfloat16), (value - high).astype(jnp.bfloat16)


def ring_parts(block, axis):
    count = lax.axis_size(axis)
    parts = [block]
    for distance in range(1, count):
        route = [(i, (i + distance) % count) for i in range(count)]
        parts.append(lax.ppermute(block, axis, route))
    return jnp.stack(parts)


def gather_owners(block):
    inner = ring_parts(block, "iface")
    outer = ring_parts(inner, "sub")
    return outer.reshape((-1,) + block.shape)


def ring_owner_order():
    subs, ifaces = lax.axis_size("sub"), lax.axis_size("iface")
    sub_back = (lax.axis_index("sub") - jnp.arange(subs)[:, None]) % subs
    iface_back = (lax.axis_index("iface") - jnp.arange(ifaces)[None, :]) % ifaces
    return (sub_back * ifaces + iface_back).reshape(-1)


def schur_rows(block_list, boundary, coupled, inverse, owners):
    picks = block_list.shape[0]
    block_nodes = boundary.shape[0] // picks
    nodes = owners * block_nodes
    contract = (((0,), (0,)), ((), ()))
    node = jnp.arange(nodes, dtype=jnp.int32)
    slot_node = jnp.arange(picks * block_nodes, dtype=jnp.int32)
    target = jnp.repeat(block_list, block_nodes) * block_nodes + slot_node % block_nodes
    place = (target[:, None] == node[None, :]).astype(jnp.bfloat16)

    def moved(matrix):
        rows = lax.dot_general(place, matrix, contract, preferred_element_type=jnp.float32)
        return jnp.dot(rows.astype(jnp.bfloat16), place, preferred_element_type=jnp.float32)

    if picks == owners:
        coupled = jnp.dot(coupled, place, preferred_element_type=jnp.float32).astype(jnp.bfloat16)
        boundary = moved(boundary)
    solved = jnp.dot(inverse, coupled, preferred_element_type=jnp.float32)
    solved_hi, solved_lo = split_bf16(solved)
    pulled = lax.dot_general(coupled, solved_hi, contract, preferred_element_type=jnp.float32)
    pulled = pulled + lax.dot_general(coupled, solved_lo, contract, preferred_element_type=jnp.float32)
    schur = boundary.astype(jnp.float32) - pulled
    if picks != owners:
        schur_hi, schur_lo = split_bf16(schur)
        schur = moved(schur_hi) + moved(schur_lo)
    return schur.reshape(owners, block_nodes, nodes)


def chain_weights(precond_parts, couple_parts, section_pos):
    highest = lax.Precision.HIGHEST
    sections, block_nodes = precond_parts.shape[0], precond_parts.shape[1]
    step = jnp.einsum("dij,djk->dik", precond_parts, couple_parts, precision=highest)
    eye = jnp.eye(block_nodes, dtype=jnp.float32)
    mine = [eye]
    for distance in range(1, sections):
        mine.append(-jnp.dot(mine[-1], step[distance - 1], precision=highest))
    mine = jnp.stack(mine)
    reach = (jnp.arange(sections) <= section_pos)[:, None, None]
    mine = jnp.where(reach, mine, 0.0)
    above = -jnp.einsum("ij,djk->dik", step[sections - 1], mine, precision=highest)
    above = above.at[sections - 1].add(eye)
    return mine, above


def body(
    previous, right_side, precond, couple, block_ids, iface_matrix, interior_coupling, inv_interior
):
    high = lax.Precision.HIGH
    section_pos = lax.axis_index("section")
    sections = lax.axis_size("section")
    owners = lax.axis_size(OWNERS)
    block_nodes = previous.shape[1]
    load_count = previous.shape[2]
    nodes = owners * block_nodes

    tables = jnp.concatenate(
        [previous[0], precond[0, 0].astype(jnp.float32), couple[0, 0].astype(jnp.float32)],
        axis=1,
    )
    first_rounded = gather_owners(previous[0].astype(jnp.bfloat16))
    tables = ring_parts(tables, "section")
    precond_parts = tables[:, :, load_count : load_count + block_nodes]
    couple_parts = tables[:, :, load_count + block_nodes :]
    weights_mine, weights_above = chain_weights(precond_parts, couple_parts, section_pos)
    has_above = section_pos + 1 < sections
    precond_mine = precond[0, 0].astype(jnp.float32)
    couple_above = couple_parts[sections - 1]

    spread = schur_rows(
        block_ids[0, 0], iface_matrix[0, 0], interior_coupling[0, 0], inv_interior[0, 0], owners
    )
    temps_mine = previous[0]
    temps_above = tables[sections - 1, :, :load_count]
    rhs = right_side[0]

    def known_part(temps_mine, temps_above):
        from_above = jnp.einsum("ij,il->jl", couple_above, temps_above, precision=high)
        from_above = jnp.where(has_above, from_above, 0.0)
        return temps_mine + jnp.dot(precond_mine, rhs - from_above, precision=high)

    known = known_part(temps_mine, temps_above)
    first_rounded, weights_mine, weights_above, known, spread = lax.optimization_barrier(
        (first_rounded, weights_mine, weights_above, known, spread)
    )
    rows = jnp.sum(lax.all_to_all(spread, OWNERS, 0, 0, tiled=True), axis=0)
    rows_hi, rows_lo = split_bf16(jnp.dot(precond_mine, rows, precision=lax.Precision.HIGHEST))
    node = jnp.arange(nodes, dtype=jnp.int32)
    source = jnp.repeat(ring_owner_order(), block_nodes) * block_nodes + node % block_nodes
    order = (node[:, None] == source[None, :]).astype(jnp.bfloat16)
    rows_hi = jnp.dot(rows_hi, order, preferred_element_type=jnp.float32).astype(jnp.bfloat16)
    rows_lo = jnp.dot(rows_lo, order, preferred_element_type=jnp.float32).astype(jnp.bfloat16)

    for sweep_index in range(SWEEPS):
        if sweep_index == 0:
            rounded = first_rounded
        else:
            rounded = gather_owners(temps_mine.astype(jnp.bfloat16))
            known = known_part(temps_mine, temps_above)
        rounded = rounded.reshape(nodes, load_count)
        update = known - (
            jnp.dot(rows_hi, rounded, preferred_element_type=jnp.float32)
            + jnp.dot(rows_lo, rounded, preferred_element_type=jnp.float32)
        )
        updates = ring_parts(update, "section")
        temps_mine = jnp.einsum("kij,kjl->il", weights_mine, updates, precision=high)
        temps_above = jnp.einsum("kij,kjl->il", weights_above, updates, precision=high)
    return temps_mine[None]


def solution(mesh):
    in_specs = (
        P("section", OWNERS, None),
        P("section", OWNERS, None),
        P("section", OWNERS, None, None),
        P("section", OWNERS, None, None),
        P("section", OWNERS, None),
        P("section", OWNERS, None, None),
        P("section", OWNERS, None, None),
        P("section", OWNERS, None, None),
    )
    out_specs = P("section", OWNERS, None)
    return jax.shard_map(body, mesh=mesh, in_specs=in_specs, out_specs=out_specs, check_vma=False)
```

```python
import jax
import jax.numpy as jnp
from jax import lax
from jax.sharding import PartitionSpec as P

SWEEPS = 4
OWNERS = ("sub", "iface")


def split_bf16(value):
    high = lax.reduce_precision(value, exponent_bits=8, mantissa_bits=7)
    return high.astype(jnp.bfloat16), (value - high).astype(jnp.bfloat16)


def ring_parts(block, axis):
    count = lax.axis_size(axis)
    parts = [block]
    for distance in range(1, count):
        route = [(i, (i + distance) % count) for i in range(count)]
        parts.append(lax.ppermute(block, axis, route))
    return jnp.stack(parts)


def gather_owners(block):
    inner = ring_parts(block, "iface")
    outer = ring_parts(inner, "sub")
    return outer.reshape((-1,) + block.shape)


def ring_owner_order():
    subs, ifaces = lax.axis_size("sub"), lax.axis_size("iface")
    sub_back = (lax.axis_index("sub") - jnp.arange(subs)[:, None]) % subs
    iface_back = (lax.axis_index("iface") - jnp.arange(ifaces)[None, :]) % ifaces
    return (sub_back * ifaces + iface_back).reshape(-1)


def schur_rows(block_list, boundary, coupled, inverse, owners):
    picks = block_list.shape[0]
    block_nodes = boundary.shape[0] // picks
    nodes = owners * block_nodes
    contract = (((0,), (0,)), ((), ()))
    node = jnp.arange(nodes, dtype=jnp.int32)
    slot_node = jnp.arange(picks * block_nodes, dtype=jnp.int32)
    target = jnp.repeat(block_list, block_nodes) * block_nodes + slot_node % block_nodes
    place = (target[:, None] == node[None, :]).astype(jnp.bfloat16)

    def moved(matrix):
        rows = lax.dot_general(place, matrix, contract, preferred_element_type=jnp.float32)
        return jnp.dot(rows.astype(jnp.bfloat16), place, preferred_element_type=jnp.float32)

    if picks == owners:
        coupled = jnp.dot(coupled, place, preferred_element_type=jnp.float32).astype(jnp.bfloat16)
        boundary = moved(boundary)
    solved = jnp.dot(inverse, coupled, preferred_element_type=jnp.float32)
    solved_hi, solved_lo = split_bf16(solved)
    pulled = lax.dot_general(coupled, solved_hi, contract, preferred_element_type=jnp.float32)
    pulled = pulled + lax.dot_general(coupled, solved_lo, contract, preferred_element_type=jnp.float32)
    schur = boundary.astype(jnp.float32) - pulled
    if picks != owners:
        schur_hi, schur_lo = split_bf16(schur)
        schur = moved(schur_hi) + moved(schur_lo)
    return schur.reshape(owners, block_nodes, nodes)


def chain_weights(precond_parts, couple_parts, section_pos):
    highest = lax.Precision.HIGHEST
    sections, block_nodes = precond_parts.shape[0], precond_parts.shape[1]
    step = jnp.einsum("dij,djk->dik", precond_parts, couple_parts, precision=highest)
    eye = jnp.eye(block_nodes, dtype=jnp.float32)
    mine = [eye]
    for distance in range(1, sections):
        mine.append(-jnp.dot(mine[-1], step[distance - 1], precision=highest))
    mine = jnp.stack(mine)
    reach = (jnp.arange(sections) <= section_pos)[:, None, None]
    mine = jnp.where(reach, mine, 0.0)
    above = -jnp.einsum("ij,djk->dik", step[sections - 1], mine, precision=highest)
    above = above.at[sections - 1].add(eye)
    return mine, above


def body(
    previous, right_side, precond, couple, block_ids, iface_matrix, interior_coupling, inv_interior
):
    high = lax.Precision.HIGH
    section_pos = lax.axis_index("section")
    sections = lax.axis_size("section")
    owners = lax.axis_size(OWNERS)
    block_nodes = previous.shape[1]
    load_count = previous.shape[2]
    nodes = owners * block_nodes

    tables = jnp.concatenate(
        [previous[0], precond[0, 0].astype(jnp.float32), couple[0, 0].astype(jnp.float32)],
        axis=1,
    )
    first_rounded = gather_owners(previous[0].astype(jnp.bfloat16))
    tables = ring_parts(tables, "section")
    precond_parts = tables[:, :, load_count : load_count + block_nodes]
    couple_parts = tables[:, :, load_count + block_nodes :]
    weights_mine, weights_above = chain_weights(precond_parts, couple_parts, section_pos)
    has_above = section_pos + 1 < sections
    precond_mine = precond[0, 0].astype(jnp.float32)
    couple_above = couple_parts[sections - 1]

    spread = schur_rows(
        block_ids[0, 0], iface_matrix[0, 0], interior_coupling[0, 0], inv_interior[0, 0], owners
    )
    temps_mine = previous[0]
    temps_above = tables[sections - 1, :, :load_count]
    rhs = right_side[0]

    def known_part(temps_mine, temps_above):
        from_above = jnp.einsum("ij,il->jl", couple_above, temps_above, precision=high)
        from_above = jnp.where(has_above, from_above, 0.0)
        return temps_mine + jnp.dot(precond_mine, rhs - from_above, precision=high)

    known = known_part(temps_mine, temps_above)
    first_rounded, weights_mine, weights_above, known, spread = lax.optimization_barrier(
        (first_rounded, weights_mine, weights_above, known, spread)
    )
    received = lax.all_to_all(spread, OWNERS, 0, 0, tiled=True).reshape(nodes, nodes)
    precond_tiled = jnp.tile(precond_mine, (1, owners))
    rows = jnp.dot(precond_tiled, received, precision=lax.Precision.HIGHEST)
    rows_hi, rows_lo = split_bf16(rows)
    node = jnp.arange(nodes, dtype=jnp.int32)
    source = jnp.repeat(ring_owner_order(), block_nodes) * block_nodes + node % block_nodes
    order = (node[:, None] == source[None, :]).astype(jnp.bfloat16)
    rows_hi = jnp.dot(rows_hi, order, preferred_element_type=jnp.float32).astype(jnp.bfloat16)
    rows_lo = jnp.dot(rows_lo, order, preferred_element_type=jnp.float32).astype(jnp.bfloat16)

    for sweep_index in range(SWEEPS):
        if sweep_index == 0:
            rounded = first_rounded
        else:
            rounded = gather_owners(temps_mine.astype(jnp.bfloat16))
            known = known_part(temps_mine, temps_above)
        rounded = rounded.reshape(nodes, load_count)
        update = known - (
            jnp.dot(rows_hi, rounded, preferred_element_type=jnp.float32)
            + jnp.dot(rows_lo, rounded, preferred_element_type=jnp.float32)
        )
        updates = ring_parts(update, "section")
        temps_mine = jnp.einsum("kij,kjl->il", weights_mine, updates, precision=high)
        temps_above = jnp.einsum("kij,kjl->il", weights_above, updates, precision=high)
    return temps_mine[None]


def solution(mesh):
    in_specs = (
        P("section", OWNERS, None),
        P("section", OWNERS, None),
        P("section", OWNERS, None, None),
        P("section", OWNERS, None, None),
        P("section", OWNERS, None),
        P("section", OWNERS, None, None),
        P("section", OWNERS, None, None),
        P("section", OWNERS, None, None),
    )
    out_specs = P("section", OWNERS, None)
    return jax.shard_map(body, mesh=mesh, in_specs=in_specs, out_specs=out_specs, check_vma=False)
```

```python
import jax
import jax.numpy as jnp
from jax import lax
from jax.sharding import PartitionSpec as P

SWEEPS = 4
OWNERS = ("sub", "iface")


def split_bf16(value):
    high = lax.reduce_precision(value, exponent_bits=8, mantissa_bits=7)
    return high.astype(jnp.bfloat16), (value - high).astype(jnp.bfloat16)


def ring_parts(block, axis):
    count = lax.axis_size(axis)
    parts = [block]
    for distance in range(1, count):
        route = [(i, (i + distance) % count) for i in range(count)]
        parts.append(lax.ppermute(block, axis, route))
    return jnp.stack(parts)


def gather_owners(block):
    inner = ring_parts(block, "sub")
    outer = ring_parts(inner, "iface")
    return outer.reshape((-1,) + block.shape)


def ring_owner_order():
    subs, ifaces = lax.axis_size("sub"), lax.axis_size("iface")
    iface_back = (lax.axis_index("iface") - jnp.arange(ifaces)[:, None]) % ifaces
    sub_back = (lax.axis_index("sub") - jnp.arange(subs)[None, :]) % subs
    return (sub_back * ifaces + iface_back).reshape(-1)


def schur_rows(block_list, boundary, coupled, inverse, owners):
    picks = block_list.shape[0]
    block_nodes = boundary.shape[0] // picks
    nodes = owners * block_nodes
    contract = (((0,), (0,)), ((), ()))
    node = jnp.arange(nodes, dtype=jnp.int32)
    slot_node = jnp.arange(picks * block_nodes, dtype=jnp.int32)
    target = jnp.repeat(block_list, block_nodes) * block_nodes + slot_node % block_nodes
    place = (target[:, None] == node[None, :]).astype(jnp.bfloat16)

    def moved(matrix):
        rows = lax.dot_general(place, matrix, contract, preferred_element_type=jnp.float32)
        return jnp.dot(rows.astype(jnp.bfloat16), place, preferred_element_type=jnp.float32)

    if picks == owners:
        coupled = jnp.dot(coupled, place, preferred_element_type=jnp.float32).astype(jnp.bfloat16)
        boundary = moved(boundary)
    solved = jnp.dot(inverse, coupled, preferred_element_type=jnp.float32)
    solved_hi, solved_lo = split_bf16(solved)
    pulled = lax.dot_general(coupled, solved_hi, contract, preferred_element_type=jnp.float32)
    pulled = pulled + lax.dot_general(coupled, solved_lo, contract, preferred_element_type=jnp.float32)
    schur = boundary.astype(jnp.float32) - pulled
    if picks != owners:
        schur_hi, schur_lo = split_bf16(schur)
        schur = moved(schur_hi) + moved(schur_lo)
    return schur.reshape(owners, block_nodes, nodes)


def chain_weights(precond_parts, couple_parts, section_pos):
    highest = lax.Precision.HIGHEST
    sections, block_nodes = precond_parts.shape[0], precond_parts.shape[1]
    step = jnp.einsum("dij,djk->dik", precond_parts, couple_parts, precision=highest)
    eye = jnp.eye(block_nodes, dtype=jnp.float32)
    mine = [eye]
    for distance in range(1, sections):
        mine.append(-jnp.dot(mine[-1], step[distance - 1], precision=highest))
    mine = jnp.stack(mine)
    reach = (jnp.arange(sections) <= section_pos)[:, None, None]
    mine = jnp.where(reach, mine, 0.0)
    above = -jnp.einsum("ij,djk->dik", step[sections - 1], mine, precision=highest)
    above = above.at[sections - 1].add(eye)
    return mine, above


def body(
    previous, right_side, precond, couple, block_ids, iface_matrix, interior_coupling, inv_interior
):
    high = lax.Precision.HIGH
    section_pos = lax.axis_index("section")
    sections = lax.axis_size("section")
    owners = lax.axis_size(OWNERS)
    block_nodes = previous.shape[1]
    load_count = previous.shape[2]
    nodes = owners * block_nodes

    tables = jnp.concatenate(
        [previous[0], precond[0, 0].astype(jnp.float32), couple[0, 0].astype(jnp.float32)],
        axis=1,
    )
    first_rounded = gather_owners(previous[0].astype(jnp.bfloat16))
    tables = ring_parts(tables, "section")
    precond_parts = tables[:, :, load_count : load_count + block_nodes]
    couple_parts = tables[:, :, load_count + block_nodes :]
    weights_mine, weights_above = chain_weights(precond_parts, couple_parts, section_pos)
    has_above = section_pos + 1 < sections
    precond_mine = precond[0, 0].astype(jnp.float32)
    couple_above = couple_parts[sections - 1]

    spread = schur_rows(
        block_ids[0, 0], iface_matrix[0, 0], interior_coupling[0, 0], inv_interior[0, 0], owners
    )
    temps_mine = previous[0]
    temps_above = tables[sections - 1, :, :load_count]
    rhs = right_side[0]

    def known_part(temps_mine, temps_above):
        from_above = jnp.einsum("ij,il->jl", couple_above, temps_above, precision=high)
        from_above = jnp.where(has_above, from_above, 0.0)
        return temps_mine + jnp.dot(precond_mine, rhs - from_above, precision=high)

    known = known_part(temps_mine, temps_above)
    first_rounded, weights_mine, weights_above, known, spread = lax.optimization_barrier(
        (first_rounded, weights_mine, weights_above, known, spread)
    )
    rows = jnp.sum(lax.all_to_all(spread, OWNERS, 0, 0, tiled=True), axis=0)
    rows_hi, rows_lo = split_bf16(jnp.dot(precond_mine, rows, precision=lax.Precision.HIGHEST))
    node = jnp.arange(nodes, dtype=jnp.int32)
    source = jnp.repeat(ring_owner_order(), block_nodes) * block_nodes + node % block_nodes
    order = (node[:, None] == source[None, :]).astype(jnp.bfloat16)
    rows_hi = jnp.dot(rows_hi, order, preferred_element_type=jnp.float32).astype(jnp.bfloat16)
    rows_lo = jnp.dot(rows_lo, order, preferred_element_type=jnp.float32).astype(jnp.bfloat16)

    for sweep_index in range(SWEEPS):
        if sweep_index == 0:
            rounded = first_rounded
        else:
            rounded = gather_owners(temps_mine.astype(jnp.bfloat16))
            known = known_part(temps_mine, temps_above)
        rounded = rounded.reshape(nodes, load_count)
        update = known - (
            jnp.dot(rows_hi, rounded, preferred_element_type=jnp.float32)
            + jnp.dot(rows_lo, rounded, preferred_element_type=jnp.float32)
        )
        updates = ring_parts(update, "section")
        temps_mine = jnp.einsum("kij,kjl->il", weights_mine, updates, precision=high)
        temps_above = jnp.einsum("kij,kjl->il", weights_above, updates, precision=high)
    return temps_mine[None]


def solution(mesh):
    in_specs = (
        P("section", OWNERS, None),
        P("section", OWNERS, None),
        P("section", OWNERS, None, None),
        P("section", OWNERS, None, None),
        P("section", OWNERS, None),
        P("section", OWNERS, None, None),
        P("section", OWNERS, None, None),
        P("section", OWNERS, None, None),
    )
    out_specs = P("section", OWNERS, None)
    return jax.shard_map(body, mesh=mesh, in_specs=in_specs, out_specs=out_specs, check_vma=False)
```

```python
import jax
import jax.numpy as jnp
from jax import lax
from jax.sharding import PartitionSpec as P

SWEEPS = 4
OWNERS = ("sub", "iface")


def split_bf16(value):
    high = lax.reduce_precision(value, exponent_bits=8, mantissa_bits=7)
    return high.astype(jnp.bfloat16), (value - high).astype(jnp.bfloat16)


def ring_parts(block, axis):
    count = lax.axis_size(axis)
    parts = [block]
    for distance in range(1, count):
        route = [(i, (i + distance) % count) for i in range(count)]
        parts.append(lax.ppermute(block, axis, route))
    return jnp.stack(parts)


def gather_owners(block):
    inner = ring_parts(block, "iface")
    outer = ring_parts(inner, "sub")
    return outer.reshape((-1,) + block.shape)


def ring_owner_order():
    subs, ifaces = lax.axis_size("sub"), lax.axis_size("iface")
    sub_back = (lax.axis_index("sub") - jnp.arange(subs)[:, None]) % subs
    iface_back = (lax.axis_index("iface") - jnp.arange(ifaces)[None, :]) % ifaces
    return (sub_back * ifaces + iface_back).reshape(-1)


def schur_rows(block_list, boundary, coupled, inverse, owners):
    picks = block_list.shape[0]
    block_nodes = boundary.shape[0] // picks
    nodes = owners * block_nodes
    contract = (((0,), (0,)), ((), ()))
    node = jnp.arange(nodes, dtype=jnp.int32)
    slot_node = jnp.arange(picks * block_nodes, dtype=jnp.int32)
    target = jnp.repeat(block_list, block_nodes) * block_nodes + slot_node % block_nodes
    place = (target[:, None] == node[None, :]).astype(jnp.bfloat16)

    def moved(matrix):
        rows = lax.dot_general(place, matrix, contract, preferred_element_type=jnp.float32)
        return jnp.dot(rows.astype(jnp.bfloat16), place, preferred_element_type=jnp.float32)

    if picks == owners:
        coupled = jnp.dot(coupled, place, preferred_element_type=jnp.float32).astype(jnp.bfloat16)
        boundary = moved(boundary)
    solved = jnp.dot(inverse, coupled, preferred_element_type=jnp.float32)
    solved_hi, solved_lo = split_bf16(solved)
    pulled = lax.dot_general(coupled, solved_hi, contract, preferred_element_type=jnp.float32)
    pulled = pulled + lax.dot_general(coupled, solved_lo, contract, preferred_element_type=jnp.float32)
    schur = boundary.astype(jnp.float32) - pulled
    if picks != owners:
        schur_hi, schur_lo = split_bf16(schur)
        schur = moved(schur_hi) + moved(schur_lo)
    return schur.reshape(owners, block_nodes, nodes)


def chain_weights(precond_parts, couple_parts, section_pos):
    highest = lax.Precision.HIGHEST
    sections, block_nodes = precond_parts.shape[0], precond_parts.shape[1]
    step = jnp.einsum("dij,djk->dik", precond_parts, couple_parts, precision=highest)
    eye = jnp.eye(block_nodes, dtype=jnp.float32)
    mine = [eye]
    for distance in range(1, sections):
        mine.append(-jnp.dot(mine[-1], step[distance - 1], precision=highest))
    mine = jnp.stack(mine)
    reach = (jnp.arange(sections) <= section_pos)[:, None, None]
    mine = jnp.where(reach, mine, 0.0)
    above = -jnp.einsum("ij,djk->dik", step[sections - 1], mine, precision=highest)
    above = above.at[sections - 1].add(eye)
    return mine, above


def body(
    previous, right_side, precond, couple, block_ids, iface_matrix, interior_coupling, inv_interior
):
    high = lax.Precision.HIGH
    section_pos = lax.axis_index("section")
    sections = lax.axis_size("section")
    owners = lax.axis_size(OWNERS)
    block_nodes = previous.shape[1]
    load_count = previous.shape[2]
    nodes = owners * block_nodes

    tables = jnp.concatenate(
        [previous[0], precond[0, 0].astype(jnp.float32), couple[0, 0].astype(jnp.float32)],
        axis=1,
    )
    first_rounded = gather_owners(previous[0].astype(jnp.bfloat16))
    tables = ring_parts(tables, "section")
    precond_parts = tables[:, :, load_count : load_count + block_nodes]
    couple_parts = tables[:, :, load_count + block_nodes :]
    weights_mine, weights_above = chain_weights(precond_parts, couple_parts, section_pos)
    has_above = section_pos + 1 < sections
    precond_mine = precond[0, 0].astype(jnp.float32)
    couple_above = couple_parts[sections - 1]

    spread = schur_rows(
        block_ids[0, 0], iface_matrix[0, 0], interior_coupling[0, 0], inv_interior[0, 0], owners
    )
    temps_mine = previous[0]
    temps_above = tables[sections - 1, :, :load_count]
    rhs = right_side[0]

    def known_part(temps_mine, temps_above):
        from_above = jnp.einsum("ij,il->jl", couple_above, temps_above, precision=high)
        from_above = jnp.where(has_above, from_above, 0.0)
        return temps_mine + jnp.dot(precond_mine, rhs - from_above, precision=high)

    known = known_part(temps_mine, temps_above)
    node = jnp.arange(nodes, dtype=jnp.int32)
    source = jnp.repeat(ring_owner_order(), block_nodes) * block_nodes + node % block_nodes
    order = (node[:, None] == source[None, :]).astype(jnp.bfloat16)
    first_nodes = jnp.dot(order, first_rounded.reshape(nodes, load_count), preferred_element_type=jnp.float32)
    first_nodes = first_nodes.astype(jnp.bfloat16)
    first_nodes, weights_mine, weights_above, known, spread = lax.optimization_barrier(
        (first_nodes, weights_mine, weights_above, known, spread)
    )
    rows = jnp.sum(lax.all_to_all(spread, OWNERS, 0, 0, tiled=True), axis=0)
    node_hi, node_lo = split_bf16(jnp.dot(precond_mine, rows, precision=lax.Precision.HIGHEST))
    rows_hi = jnp.dot(node_hi, order, preferred_element_type=jnp.float32).astype(jnp.bfloat16)
    rows_lo = jnp.dot(node_lo, order, preferred_element_type=jnp.float32).astype(jnp.bfloat16)

    for sweep_index in range(SWEEPS):
        if sweep_index == 0:
            update = known - (
                jnp.dot(node_hi, first_nodes, preferred_element_type=jnp.float32)
                + jnp.dot(node_lo, first_nodes, preferred_element_type=jnp.float32)
            )
        else:
            rounded = gather_owners(temps_mine.astype(jnp.bfloat16))
            known = known_part(temps_mine, temps_above)
            rounded = rounded.reshape(nodes, load_count)
            update = known - (
                jnp.dot(rows_hi, rounded, preferred_element_type=jnp.float32)
                + jnp.dot(rows_lo, rounded, preferred_element_type=jnp.float32)
            )
        updates = ring_parts(update, "section")
        temps_mine = jnp.einsum("kij,kjl->il", weights_mine, updates, precision=high)
        temps_above = jnp.einsum("kij,kjl->il", weights_above, updates, precision=high)
    return temps_mine[None]


def solution(mesh):
    in_specs = (
        P("section", OWNERS, None),
        P("section", OWNERS, None),
        P("section", OWNERS, None, None),
        P("section", OWNERS, None, None),
        P("section", OWNERS, None),
        P("section", OWNERS, None, None),
        P("section", OWNERS, None, None),
        P("section", OWNERS, None, None),
    )
    out_specs = P("section", OWNERS, None)
    return jax.shard_map(body, mesh=mesh, in_specs=in_specs, out_specs=out_specs, check_vma=False)
```

```python
import jax
import jax.numpy as jnp
from jax import lax
from jax.sharding import PartitionSpec as P

SWEEPS = 4
OWNERS = ("sub", "iface")


def split_bf16(value):
    high = lax.reduce_precision(value, exponent_bits=8, mantissa_bits=7)
    return high.astype(jnp.bfloat16), (value - high).astype(jnp.bfloat16)


def ring_parts(block, axis):
    count = lax.axis_size(axis)
    parts = [block]
    for distance in range(1, count):
        route = [(i, (i + distance) % count) for i in range(count)]
        parts.append(lax.ppermute(block, axis, route))
    return jnp.stack(parts)


def gather_owners(block):
    inner = ring_parts(block, "iface")
    outer = ring_parts(inner, "sub")
    return outer.reshape((-1,) + block.shape)


def ring_owner_order():
    subs, ifaces = lax.axis_size("sub"), lax.axis_size("iface")
    sub_back = (lax.axis_index("sub") - jnp.arange(subs)[:, None]) % subs
    iface_back = (lax.axis_index("iface") - jnp.arange(ifaces)[None, :]) % ifaces
    return (sub_back * ifaces + iface_back).reshape(-1)


def schur_rows(block_list, boundary, coupled, inverse, owners):
    picks = block_list.shape[0]
    block_nodes = boundary.shape[0] // picks
    nodes = owners * block_nodes
    contract = (((0,), (0,)), ((), ()))
    node = jnp.arange(nodes, dtype=jnp.int32)
    slot_node = jnp.arange(picks * block_nodes, dtype=jnp.int32)
    target = jnp.repeat(block_list, block_nodes) * block_nodes + slot_node % block_nodes
    place = (target[:, None] == node[None, :]).astype(jnp.bfloat16)

    def moved(matrix):
        rows = lax.dot_general(place, matrix, contract, preferred_element_type=jnp.float32)
        return jnp.dot(rows.astype(jnp.bfloat16), place, preferred_element_type=jnp.float32)

    if picks == owners:
        coupled = jnp.dot(coupled, place, preferred_element_type=jnp.float32).astype(jnp.bfloat16)
        boundary = moved(boundary)
    solved = jnp.dot(inverse, coupled, preferred_element_type=jnp.float32)
    solved_hi, solved_lo = split_bf16(solved)
    pulled = lax.dot_general(coupled, solved_hi, contract, preferred_element_type=jnp.float32)
    pulled = pulled + lax.dot_general(coupled, solved_lo, contract, preferred_element_type=jnp.float32)
    schur = boundary.astype(jnp.float32) - pulled
    if picks != owners:
        schur_hi, schur_lo = split_bf16(schur)
        schur = moved(schur_hi) + moved(schur_lo)
    return schur.reshape(owners, block_nodes, nodes)


def chain_weights(precond_parts, couple_parts, section_pos):
    highest = lax.Precision.HIGHEST
    sections, block_nodes = precond_parts.shape[0], precond_parts.shape[1]
    step = jnp.einsum("dij,djk->dik", precond_parts, couple_parts, precision=highest)
    eye = jnp.eye(block_nodes, dtype=jnp.float32)
    mine = [eye]
    for distance in range(1, sections):
        mine.append(-jnp.dot(mine[-1], step[distance - 1], precision=highest))
    mine = jnp.stack(mine)
    reach = (jnp.arange(sections) <= section_pos)[:, None, None]
    mine = jnp.where(reach, mine, 0.0)
    above = -jnp.einsum("ij,djk->dik", step[sections - 1], mine, precision=highest)
    above = above.at[sections - 1].add(eye)
    return mine, above


def body(
    previous, right_side, precond, couple, block_ids, iface_matrix, interior_coupling, inv_interior
):
    high = lax.Precision.HIGH
    section_pos = lax.axis_index("section")
    sections = lax.axis_size("section")
    owners = lax.axis_size(OWNERS)
    block_nodes = previous.shape[1]
    load_count = previous.shape[2]
    nodes = owners * block_nodes

    tables = jnp.concatenate(
        [previous[0], precond[0, 0].astype(jnp.float32), couple[0, 0].astype(jnp.float32)],
        axis=1,
    )
    first_rounded = gather_owners(previous[0].astype(jnp.bfloat16))
    tables = ring_parts(tables, "section")
    precond_parts = tables[:, :, load_count : load_count + block_nodes]
    couple_parts = tables[:, :, load_count + block_nodes :]
    weights_mine, weights_above = chain_weights(precond_parts, couple_parts, section_pos)
    has_above = section_pos + 1 < sections
    precond_mine = precond[0, 0].astype(jnp.float32)
    couple_above = couple_parts[sections - 1]

    spread = schur_rows(
        block_ids[0, 0], iface_matrix[0, 0], interior_coupling[0, 0], inv_interior[0, 0], owners
    )
    temps_mine = previous[0]
    temps_above = tables[sections - 1, :, :load_count]
    rhs = right_side[0]

    def known_part(temps_mine, temps_above):
        from_above = jnp.einsum("ij,il->jl", couple_above, temps_above, precision=high)
        from_above = jnp.where(has_above, from_above, 0.0)
        return temps_mine + jnp.dot(precond_mine, rhs - from_above, precision=high)

    known = known_part(temps_mine, temps_above)
    first_rounded, weights_mine, weights_above, known, spread = lax.optimization_barrier(
        (first_rounded, weights_mine, weights_above, known, spread)
    )
    rows = jnp.sum(lax.all_to_all(spread, OWNERS, 0, 0, tiled=True), axis=0)
    rows_hi, rows_lo = split_bf16(jnp.dot(precond_mine, rows, precision=lax.Precision.HIGHEST))
    node = jnp.arange(nodes, dtype=jnp.int32)
    source = jnp.repeat(ring_owner_order(), block_nodes) * block_nodes + node % block_nodes
    order = (node[:, None] == source[None, :]).astype(jnp.bfloat16)
    rows_hi = jnp.dot(rows_hi, order, preferred_element_type=jnp.float32).astype(jnp.bfloat16)
    rows_lo = jnp.dot(rows_lo, order, preferred_element_type=jnp.float32).astype(jnp.bfloat16)

    weights_both = jnp.stack([weights_mine, weights_above])
    for sweep_index in range(SWEEPS):
        if sweep_index == 0:
            rounded = first_rounded
        else:
            rounded = gather_owners(temps_mine.astype(jnp.bfloat16))
            known = known_part(temps_mine, temps_above)
        rounded = rounded.reshape(nodes, load_count)
        update = known - (
            jnp.dot(rows_hi, rounded, preferred_element_type=jnp.float32)
            + jnp.dot(rows_lo, rounded, preferred_element_type=jnp.float32)
        )
        updates = ring_parts(update, "section")
        swept = jnp.einsum("skij,kjl->sil", weights_both, updates, precision=high)
        temps_mine, temps_above = swept[0], swept[1]
    return temps_mine[None]


def solution(mesh):
    in_specs = (
        P("section", OWNERS, None),
        P("section", OWNERS, None),
        P("section", OWNERS, None, None),
        P("section", OWNERS, None, None),
        P("section", OWNERS, None),
        P("section", OWNERS, None, None),
        P("section", OWNERS, None, None),
        P("section", OWNERS, None, None),
    )
    out_specs = P("section", OWNERS, None)
    return jax.shard_map(body, mesh=mesh, in_specs=in_specs, out_specs=out_specs, check_vma=False)
```

```python
import jax
import jax.numpy as jnp
from jax import lax
from jax.sharding import PartitionSpec as P

SWEEPS = 4
OWNERS = ("sub", "iface")


def split_bf16(value):
    high = lax.reduce_precision(value, exponent_bits=8, mantissa_bits=7)
    return high.astype(jnp.bfloat16), (value - high).astype(jnp.bfloat16)


def ring_parts(block, axis):
    count = lax.axis_size(axis)
    parts = [block]
    for distance in range(1, count):
        route = [(i, (i + distance) % count) for i in range(count)]
        parts.append(lax.ppermute(block, axis, route))
    return jnp.stack(parts)


def gather_owners(block):
    inner = ring_parts(block, "iface")
    outer = ring_parts(inner, "sub")
    return outer.reshape((-1,) + block.shape)


def ring_owner_order():
    subs, ifaces = lax.axis_size("sub"), lax.axis_size("iface")
    sub_back = (lax.axis_index("sub") - jnp.arange(subs)[:, None]) % subs
    iface_back = (lax.axis_index("iface") - jnp.arange(ifaces)[None, :]) % ifaces
    return (sub_back * ifaces + iface_back).reshape(-1)


def schur_rows(block_list, boundary, coupled, inverse, owners):
    picks = block_list.shape[0]
    block_nodes = boundary.shape[0] // picks
    nodes = owners * block_nodes
    contract = (((0,), (0,)), ((), ()))
    node = jnp.arange(nodes, dtype=jnp.int32)
    slot_node = jnp.arange(picks * block_nodes, dtype=jnp.int32)
    target = jnp.repeat(block_list, block_nodes) * block_nodes + slot_node % block_nodes
    place = (target[:, None] == node[None, :]).astype(jnp.bfloat16)

    def moved(matrix):
        rows = lax.dot_general(place, matrix, contract, preferred_element_type=jnp.float32)
        return jnp.dot(rows.astype(jnp.bfloat16), place, preferred_element_type=jnp.float32)

    if picks == owners:
        coupled = jnp.dot(coupled, place, preferred_element_type=jnp.float32).astype(jnp.bfloat16)
        boundary = moved(boundary)
    solved = jnp.dot(inverse, coupled, preferred_element_type=jnp.float32)
    solved_hi, solved_lo = split_bf16(solved)
    both = jnp.concatenate([solved_hi, solved_lo], axis=1)
    pulled = lax.dot_general(coupled, both, contract, preferred_element_type=jnp.float32)
    pulled = pulled[:, : solved.shape[1]] + pulled[:, solved.shape[1] :]
    schur = boundary.astype(jnp.float32) - pulled
    if picks != owners:
        schur_hi, schur_lo = split_bf16(schur)
        schur = moved(schur_hi) + moved(schur_lo)
    return schur.reshape(owners, block_nodes, nodes)


def chain_weights(precond_parts, couple_parts, section_pos):
    highest = lax.Precision.HIGHEST
    sections, block_nodes = precond_parts.shape[0], precond_parts.shape[1]
    step = jnp.einsum("dij,djk->dik", precond_parts, couple_parts, precision=highest)
    eye = jnp.eye(block_nodes, dtype=jnp.float32)
    mine = [eye]
    for distance in range(1, sections):
        mine.append(-jnp.dot(mine[-1], step[distance - 1], precision=highest))
    mine = jnp.stack(mine)
    reach = (jnp.arange(sections) <= section_pos)[:, None, None]
    mine = jnp.where(reach, mine, 0.0)
    above = -jnp.einsum("ij,djk->dik", step[sections - 1], mine, precision=highest)
    above = above.at[sections - 1].add(eye)
    return mine, above


def body(
    previous, right_side, precond, couple, block_ids, iface_matrix, interior_coupling, inv_interior
):
    high = lax.Precision.HIGH
    section_pos = lax.axis_index("section")
    sections = lax.axis_size("section")
    owners = lax.axis_size(OWNERS)
    block_nodes = previous.shape[1]
    load_count = previous.shape[2]
    nodes = owners * block_nodes

    tables = jnp.concatenate(
        [previous[0], precond[0, 0].astype(jnp.float32), couple[0, 0].astype(jnp.float32)],
        axis=1,
    )
    first_rounded = gather_owners(previous[0].astype(jnp.bfloat16))
    tables = ring_parts(tables, "section")
    precond_parts = tables[:, :, load_count : load_count + block_nodes]
    couple_parts = tables[:, :, load_count + block_nodes :]
    weights_mine, weights_above = chain_weights(precond_parts, couple_parts, section_pos)
    has_above = section_pos + 1 < sections
    precond_mine = precond[0, 0].astype(jnp.float32)
    couple_above = couple_parts[sections - 1]

    spread = schur_rows(
        block_ids[0, 0], iface_matrix[0, 0], interior_coupling[0, 0], inv_interior[0, 0], owners
    )
    temps_mine = previous[0]
    temps_above = tables[sections - 1, :, :load_count]
    rhs = right_side[0]

    def known_part(temps_mine, temps_above):
        from_above = jnp.einsum("ij,il->jl", couple_above, temps_above, precision=high)
        from_above = jnp.where(has_above, from_above, 0.0)
        return temps_mine + jnp.dot(precond_mine, rhs - from_above, precision=high)

    known = known_part(temps_mine, temps_above)
    first_rounded, weights_mine, weights_above, known, spread = lax.optimization_barrier(
        (first_rounded, weights_mine, weights_above, known, spread)
    )
    rows = jnp.sum(lax.all_to_all(spread, OWNERS, 0, 0, tiled=True), axis=0)
    rows_hi, rows_lo = split_bf16(jnp.dot(precond_mine, rows, precision=lax.Precision.HIGHEST))
    node = jnp.arange(nodes, dtype=jnp.int32)
    source = jnp.repeat(ring_owner_order(), block_nodes) * block_nodes + node % block_nodes
    order = (node[:, None] == source[None, :]).astype(jnp.bfloat16)
    rows_hi = jnp.dot(rows_hi, order, preferred_element_type=jnp.float32).astype(jnp.bfloat16)
    rows_lo = jnp.dot(rows_lo, order, preferred_element_type=jnp.float32).astype(jnp.bfloat16)

    for sweep_index in range(SWEEPS):
        if sweep_index == 0:
            rounded = first_rounded
        else:
            rounded = gather_owners(temps_mine.astype(jnp.bfloat16))
            known = known_part(temps_mine, temps_above)
        rounded = rounded.reshape(nodes, load_count)
        update = known - (
            jnp.dot(rows_hi, rounded, preferred_element_type=jnp.float32)
            + jnp.dot(rows_lo, rounded, preferred_element_type=jnp.float32)
        )
        updates = ring_parts(update, "section")
        temps_mine = jnp.einsum("kij,kjl->il", weights_mine, updates, precision=high)
        temps_above = jnp.einsum("kij,kjl->il", weights_above, updates, precision=high)
    return temps_mine[None]


def solution(mesh):
    in_specs = (
        P("section", OWNERS, None),
        P("section", OWNERS, None),
        P("section", OWNERS, None, None),
        P("section", OWNERS, None, None),
        P("section", OWNERS, None),
        P("section", OWNERS, None, None),
        P("section", OWNERS, None, None),
        P("section", OWNERS, None, None),
    )
    out_specs = P("section", OWNERS, None)
    return jax.shard_map(body, mesh=mesh, in_specs=in_specs, out_specs=out_specs, check_vma=False)
```
